128 devices in a mesh: seq: 16 (over x, z), chan: 8 (over y, core).
Axes of the slice: x: 4, y: 4, z: 4, core: 2. Of those that a mesh axis runs over, the one named last changes fastest.
Arguments:
- inputs: bfloat16 [32768, 1024], P('seq'), may hold values from -88 to 88
- gaps: float32 [32768], P('seq'), as said below
- rates: float32 [4096], P('chan'), as said below
- w_in: bfloat16 [1024, 4096], P(None, 'chan'), may hold values from -0.25 to 0.25
- w_out: bfloat16 [4096, 1024], P('chan'), may hold values from -0.09375 to 0.09375
- cotangent: bfloat16 [32768, 1024], P('seq'), may hold values from -48 to 48
Outputs:
- d_inputs: bfloat16 [32768, 1024], P('seq', 'chan')
- d_w_in: float32 [1024, 4096], P('seq', 'chan')
- d_w_out: float32 [4096, 1024], P('chan', 'seq')
The draws below stay inside these ranges and needn't reach their ends.
Inputs may be any that keep to these rules, and one draw needn't show every extreme that they name: `gaps`: every gap is positive; at a few positions of the whole log drawn from the seed the gap is a sizable fraction of 32768. `rates`: every rate is positive.
All inputs are finite; a program needn't handle non-finite values.
Results may differ from the reference program's by a relative error of at most 0.02.
Values may be sent and summed in bfloat16 or wider, within the bound.
No kernel may reach another device: no remote copies, remote signals or barrier semaphores. Data moves between devices by JAX's collectives and lax.ppermute only.
A program may use at most 128 MiB of HBM per device.

```python
import math
import jax
import jax.numpy as jnp
from jax import lax

DMODEL = 1024
STATE = 4096
TOK_DEV = 2048
LENGTH = 32768
N_CHAN = 8


def gap_values(key):
    local = jax.random.fold_in(key, 5)
    first, second, third = jax.random.split(local, 3)
    base = jax.random.uniform(first, (LENGTH,), jnp.float32, 0.5, 1.5)
    spots = jax.random.randint(second, (6,), 0, LENGTH)
    places = jnp.arange(LENGTH, dtype=jnp.int32)
    struck = jnp.any(places[:, None] == spots[None, :], axis=1)
    large = LENGTH * jax.random.uniform(third, (LENGTH,), jnp.float32, 0.1, 0.2)
    return jnp.where(struck, large, base).astype(jnp.float32)


def spike_factor(key, times):
    blocks = LENGTH // TOK_DEV
    pairing = jax.random.permutation(key, blocks)
    row_block = times // TOK_DEV
    col_block = jnp.arange(DMODEL, dtype=jnp.int32) // (DMODEL // blocks)
    struck = pairing[row_block][:, None] == col_block[None, :]
    return jnp.where(struck, 4.0, 1.0).astype(jnp.float32)


def noise_field(key, salt):
    local = jax.random.fold_in(key, salt)
    first, second = jax.random.split(local, 2)
    times = jnp.arange(LENGTH, dtype=jnp.int32)
    normal_draw = jax.random.normal(first, (LENGTH, DMODEL), jnp.float32)
    return jnp.clip(normal_draw, -4.0, 4.0) * spike_factor(second, times)


def draw_gaps(key, part):
    return gap_values(key)


def draw_inputs(key, part):
    values = noise_field(key, 21)
    return values.astype(jnp.bfloat16)


def draw_cotangent(key, part):
    return noise_field(key, 31).astype(jnp.bfloat16)


def draw_rates(key, part):
    first = jax.random.fold_in(key, 0)
    lowest = math.log(0.05 / LENGTH)
    values = jnp.exp(jax.random.uniform(first, (STATE,), jnp.float32, lowest, math.log(0.03)))
    return values.astype(jnp.float32)


def with_spikes(entries, own_key, source, target, parts, factor):
    def block_of(axis_at):
        return (jnp.arange(entries.shape[axis_at]) // (entries.shape[axis_at] // parts)).reshape((-1,) + (1,) * (entries.ndim - 1 - axis_at))

    near = jax.random.permutation(own_key, parts)[block_of(target)]
    second = (block_of(target) + parts // 2) % parts
    return jnp.where((block_of(source) == near) | (block_of(source) == second), factor * entries, entries)


def block_levels(stream_key, dims, shards, least, high):
    def one(axis_at, blocks):
        heights = jax.random.uniform(jax.random.fold_in(jax.random.fold_in(stream_key, 6), axis_at), (blocks,), jnp.float32, least / len(shards), high / len(shards))
        return jnp.repeat(jnp.exp(heights), dims[axis_at] // blocks).reshape((-1,) + (1,) * (len(dims) - axis_at - 1))

    factor_of = one(*shards[0])
    for cut in shards[1:]:
        factor_of = factor_of * one(*cut)
    return factor_of


def noise(own_key, extent, scale, bound, shards=(), held_as=jnp.bfloat16):
    array = jax.random.normal(own_key, extent, jnp.float32) * scale
    if len(shards) > 0:
        array = block_levels(own_key, extent, shards, -0.22, 0.18) * array
    return jnp.clip(array, min=-bound, max=bound).astype(held_as)


def noise_with(key, dims, scale, limit, pieces, heavy, held_as=jnp.bfloat16):
    drawn = scale * jax.random.normal(key, dims, jnp.float32)
    if pieces:
        drawn = drawn * block_levels(key, dims, pieces, -0.22, 0.18)
    return jnp.clip(with_spikes(drawn, jax.random.fold_in(key, 3), *heavy), -limit, limit).astype(held_as)


def setup_inputs(seed: int = 0) -> dict:
    splits = jax.random.split(jax.random.key(seed), 7)
    return {
        "inputs": draw_inputs(jax.random.fold_in(splits[6], 71), 0),
        "gaps": draw_gaps(jax.random.fold_in(splits[6], 71), 0),
        "rates": draw_rates(jax.random.fold_in(splits[6], 71), 0),
        "w_in": noise_with(splits[3], (DMODEL, STATE), DMODEL ** -0.5, 0.25, ((1, 8),), (1, 0, 8, 2.0)),
        "w_out": noise(splits[4], (STATE, DMODEL), STATE ** -0.5, 0.09375, ((0, 8),)),
        "cotangent": draw_cotangent(jax.random.fold_in(splits[6], 71), 0),
    }


def link(earlier, later):
    return (earlier[0] * later[0], later[0] * earlier[1] + later[1])

def reference(inputs, gaps, rates, w_in, w_out, cotangent):
    width = STATE // N_CHAN
    factor = 1.0 / math.sqrt(LENGTH)

    def group(accum, index):
        start = (index * width).astype(jnp.int32)
        w_part = lax.dynamic_slice_in_dim(w_in, start, width, 1)
        o_part = lax.dynamic_slice_in_dim(w_out, start, width, 0)
        r_part = lax.dynamic_slice_in_dim(rates, start, width, 0)
        decay = jnp.exp(-gaps[:, None] * r_part[None, :])
        gain = jnp.sqrt(-jnp.expm1(-2.0 * gaps[:, None] * r_part[None, :]))
        drive = gain * jnp.dot(inputs, w_part, preferred_element_type=jnp.float32)
        state = lax.associative_scan(link, (decay, drive), axis=0)[1]
        upstream = lax.dot_general(cotangent, o_part, (((1,), (1,)), ((), ())), preferred_element_type=jnp.float32)
        shifted = jnp.concatenate([decay[1:], jnp.ones((1, width), jnp.float32)], 0)
        adjoint = lax.associative_scan(link, (shifted[::-1], upstream[::-1]), axis=0)[1][::-1]
        drive_grad = (gain * adjoint).astype(jnp.bfloat16)
        state_low = state.astype(jnp.bfloat16)
        grad_out = lax.dot_general(state_low, cotangent, (((0,), (0,)), ((), ())), preferred_element_type=jnp.float32) * factor
        grad_in = lax.dot_general(inputs, drive_grad, (((0,), (0,)), ((), ())), preferred_element_type=jnp.float32) * factor
        partial_low = lax.dot_general(drive_grad, w_part, (((1,), (1,)), ((), ())), preferred_element_type=jnp.float32).astype(jnp.bfloat16)
        partial_low = lax.optimization_barrier(partial_low)
        return (accum + partial_low.astype(jnp.float32), (grad_in, grad_out))
    start_acc = jnp.zeros((LENGTH, DMODEL), jnp.float32)
    total, stacked = lax.scan(group, start_acc, jnp.arange(N_CHAN, dtype=jnp.int32))
    grad_in, grad_out = stacked
    d_w_in = jnp.transpose(grad_in, (1, 0, 2)).reshape(DMODEL, STATE)
    d_w_out = grad_out.reshape(STATE, DMODEL)
    return (total.astype(jnp.bfloat16), d_w_in, d_w_out)
```

```python
import math

import jax
import jax.numpy as jnp
from jax import lax
from jax.experimental import pallas as pl
from jax.experimental.pallas import tpu as pltpu
from jax.sharding import PartitionSpec as P

SEGMENTS = 8
LANES = 128
UNROLL = 8


def _summary_kernel(g_ref, gn_ref, r_ref, *refs):
    chunks = (len(refs) - 4) // 2
    drive_refs = refs[:chunks]
    up_refs = refs[chunks:2 * chunks]
    fa_ref, fb_ref, ba_ref, bb_ref = refs[2 * chunks:]
    steps, segs, _ = g_ref.shape
    rs = [r_ref[:, pl.ds(k * LANES, LANES)] for k in range(chunks)]
    ones = tuple(jnp.ones((segs, LANES), jnp.float32) for _ in range(chunks))
    zeros = tuple(jnp.zeros((segs, LANES), jnp.float32) for _ in range(chunks))

    def fwd(i, carry):
        a, b = carry
        g = g_ref[i]
        new_a, new_b = [], []
        for k in range(chunks):
            d = jnp.exp(-(g * rs[k]))
            x = drive_refs[k][pl.ds(i, segs, stride=steps), :]
            new_a.append(a[k] * d)
            new_b.append(d * b[k] + x)
        return (tuple(new_a), tuple(new_b))

    a, b = lax.fori_loop(0, steps, fwd, (ones, zeros), unroll=UNROLL)
    for k in range(chunks):
        fa_ref[:, pl.ds(k * LANES, LANES)] = a[k]
        fb_ref[:, pl.ds(k * LANES, LANES)] = b[k]

    def bwd(j, carry):
        a, b = carry
        i = steps - 1 - j
        g = gn_ref[i]
        new_a, new_b = [], []
        for k in range(chunks):
            e = jnp.exp(-(g * rs[k]))
            u = up_refs[k][pl.ds(i, segs, stride=steps), :]
            new_a.append(a[k] * e)
            new_b.append(e * b[k] + u)
        return (tuple(new_a), tuple(new_b))

    a, b = lax.fori_loop(0, steps, bwd, (ones, zeros), unroll=UNROLL)
    for k in range(chunks):
        ba_ref[:, pl.ds(k * LANES, LANES)] = a[k]
        bb_ref[:, pl.ds(k * LANES, LANES)] = b[k]


def _sweep_kernel(g_ref, gn_ref, r_ref, if_ref, ib_ref, *refs):
    chunks = (len(refs) - 2) // 2
    drive_refs = refs[:chunks]
    up_refs = refs[chunks:2 * chunks]
    st_ref, adj_ref = refs[2 * chunks:]
    steps, segs, _ = g_ref.shape
    rs = [r_ref[:, pl.ds(k * LANES, LANES)] for k in range(chunks)]

    def fwd(i, b):
        g = g_ref[i]
        out = []
        for k in range(chunks):
            d = jnp.exp(-(g * rs[k]))
            v = d * b[k] + drive_refs[k][pl.ds(i, segs, stride=steps), :]
            st_ref[k, pl.ds(i, segs, stride=steps), :] = v
            out.append(v)
        return tuple(out)

    init = tuple(if_ref[:, pl.ds(k * LANES, LANES)] for k in range(chunks))
    lax.fori_loop(0, steps, fwd, init, unroll=UNROLL)

    def bwd(j, b):
        i = steps - 1 - j
        g = gn_ref[i]
        out = []
        for k in range(chunks):
            e = jnp.exp(-(g * rs[k]))
            v = e * b[k] + up_refs[k][pl.ds(i, segs, stride=steps), :]
            adj_ref[k, pl.ds(i, segs, stride=steps), :] = v
            out.append(v)
        return tuple(out)

    init = tuple(ib_ref[:, pl.ds(k * LANES, LANES)] for k in range(chunks))
    lax.fori_loop(0, steps, bwd, init, unroll=UNROLL)


def _column_specs(total, width):
    return [pl.BlockSpec((total, LANES), lambda j, k=k: (0, k)) for k in range(width // LANES)]


def _whole(shape):
    return pl.BlockSpec(shape, lambda j: (0,) * len(shape))


def local_summaries(g3, gn3, rates2, drive, up):
    total, width = drive.shape
    steps, segs, _ = g3.shape
    chunks = width // LANES
    cols = _column_specs(total, width)
    seg_shape = jax.ShapeDtypeStruct((segs, width), jnp.float32)
    return pl.pallas_call(
        _summary_kernel,
        grid=(1,),
        in_specs=[_whole(g3.shape), _whole(gn3.shape), _whole(rates2.shape)] + cols + cols,
        out_specs=[_whole((segs, width))] * 4,
        out_shape=[seg_shape] * 4,
        compiler_params=pltpu.CompilerParams(vmem_limit_bytes=48 * 1024 * 1024),
    )(g3, gn3, rates2, *([drive] * chunks), *([up] * chunks))


def sweeps(g3, gn3, rates2, drive, up, init_f, init_b):
    total, width = drive.shape
    steps, segs, _ = g3.shape
    chunks = width // LANES
    cols = _column_specs(total, width)
    full = jax.ShapeDtypeStruct((chunks, total, LANES), jnp.float32)
    return pl.pallas_call(
        _sweep_kernel,
        grid=(1,),
        in_specs=[_whole(g3.shape), _whole(gn3.shape), _whole(rates2.shape),
                  _whole(init_f.shape), _whole(init_b.shape)] + cols + cols,
        out_specs=[_whole(full.shape)] * 2,
        out_shape=[full, full],
        compiler_params=pltpu.CompilerParams(vmem_limit_bytes=48 * 1024 * 1024),
    )(g3, gn3, rates2, init_f, init_b, *([drive] * chunks), *([up] * chunks))


def local(inputs, gaps, rates, w_in, w_out, cotangent):
    total = inputs.shape[0]
    width = rates.shape[0]
    segs = SEGMENTS
    steps = total // segs
    peers = lax.axis_size("seq")
    place = lax.axis_index("seq")
    factor = 1.0 / math.sqrt(total * peers)

    gain = jnp.sqrt(-jnp.expm1(-2.0 * gaps[:, None] * rates[None, :]))
    drive = gain * jnp.dot(inputs, w_in, preferred_element_type=jnp.float32)
    upstream = lax.dot_general(
        cotangent, w_out, (((1,), (1,)), ((), ())), preferred_element_type=jnp.float32
    )
    gaps_next = jnp.concatenate([gaps[1:], jnp.zeros((1,), jnp.float32)], 0)
    g3 = gaps.reshape(segs, steps).T[:, :, None]
    gn3 = gaps_next.reshape(segs, steps).T[:, :, None]
    rates2 = rates[None, :]

    fa, fb, ba, bb = local_summaries(g3, gn3, rates2, drive, up=upstream)

    end_state = jnp.zeros((width,), jnp.float32)
    block_decay = jnp.ones((width,), jnp.float32)
    for s in range(segs):
        end_state = fb[s] + fa[s] * end_state
        block_decay = block_decay * fa[s]
    first_adj = jnp.zeros((width,), jnp.float32)
    for s in reversed(range(segs)):
        first_adj = bb[s] + ba[s] * first_adj
    start_adj = jnp.exp(-gaps[0] * rates) * first_adj

    gathered = lax.all_gather(jnp.stack([block_decay, end_state, start_adj], 0), "seq")
    carry_in = jnp.zeros((width,), jnp.float32)
    for q in range(peers):
        new = gathered[q, 1] + gathered[q, 0] * carry_in
        carry_in = jnp.where(q < place, new, carry_in)
    right_in = jnp.zeros((width,), jnp.float32)
    for q in reversed(range(peers)):
        new = gathered[q, 2] + gathered[q, 0] * right_in
        right_in = jnp.where(q > place, new, right_in)

    inits_f = []
    e = carry_in
    for s in range(segs):
        inits_f.append(e)
        e = fb[s] + fa[s] * e
    inits_b = [None] * segs
    v = right_in
    for s in reversed(range(segs)):
        inits_b[s] = v
        v = bb[s] + ba[s] * v
    init_f = jnp.stack(inits_f, 0)
    init_b = jnp.stack(inits_b, 0)

    state, adjoint = sweeps(g3, gn3, rates2, drive, upstream, init_f, init_b)
    chunks = width // LANES
    gain3 = gain.reshape(total, chunks, LANES).transpose(1, 0, 2)
    drive_grad = (gain3 * adjoint).astype(jnp.bfloat16)
    state_low = state.astype(jnp.bfloat16)
    d_w_in = lax.psum_scatter(
        (
            lax.dot_general(
                inputs, drive_grad, (((0,), (1,)), ((), ())), preferred_element_type=jnp.float32
            ).reshape(inputs.shape[1], width)
            * factor
        ).astype(jnp.bfloat16),
        "seq",
        scatter_dimension=0,
        tiled=True,
    ).astype(jnp.float32)
    out_term = (
        lax.dot_general(
            state_low, cotangent, (((1,), (0,)), ((), ())), preferred_element_type=jnp.float32
        ).reshape(width, cotangent.shape[1])
        * factor
    )
    d_w_out = lax.psum_scatter(
        out_term.astype(jnp.bfloat16), "seq", scatter_dimension=1, tiled=True
    ).astype(jnp.float32)
    w_in3 = w_in.reshape(w_in.shape[0], chunks, LANES)
    partial_value = lax.dot_general(
        drive_grad, w_in3, (((0, 2), (1, 2)), ((), ())), preferred_element_type=jnp.float32
    )
    d_inputs = lax.psum_scatter(
        partial_value.astype(jnp.bfloat16), "chan", scatter_dimension=1, tiled=True
    )
    return (d_inputs, d_w_in, d_w_out)


def solution(mesh):
    placed = (P("seq", None), P("seq"), P("chan"), P(None, "chan"), P("chan", None), P("seq", None))
    return jax.shard_map(
        local,
        mesh=mesh,
        in_specs=placed,
        out_specs=(P("seq", "chan"), P("seq", "chan"), P("chan", "seq")),
        check_vma=False,
    )
```

```python
import math

import jax
import jax.numpy as jnp
from jax import lax
from jax.experimental import pallas as pl
from jax.experimental.pallas import tpu as pltpu
from jax.sharding import Mesh, PartitionSpec as P

SEGMENTS = 8
LANES = 128
UNROLL = 8


def _summary_kernel(g_ref, gn_ref, r_ref, *refs):
    chunks = (len(refs) - 4) // 2
    drive_refs = refs[:chunks]
    up_refs = refs[chunks:2 * chunks]
    fa_ref, fb_ref, ba_ref, bb_ref = refs[2 * chunks:]
    steps, segs, _ = g_ref.shape
    rs = [r_ref[:, pl.ds(k * LANES, LANES)] for k in range(chunks)]
    ones = tuple(jnp.ones((segs, LANES), jnp.float32) for _ in range(chunks))
    zeros = tuple(jnp.zeros((segs, LANES), jnp.float32) for _ in range(chunks))

    def fwd(i, carry):
        a, b = carry
        g = g_ref[i]
        new_a, new_b = [], []
        for k in range(chunks):
            d = jnp.exp(-(g * rs[k]))
            x = drive_refs[k][pl.ds(i, segs, stride=steps), :]
            new_a.append(a[k] * d)
            new_b.append(d * b[k] + x)
        return (tuple(new_a), tuple(new_b))

    a, b = lax.fori_loop(0, steps, fwd, (ones, zeros), unroll=UNROLL)
    for k in range(chunks):
        fa_ref[:, pl.ds(k * LANES, LANES)] = a[k]
        fb_ref[:, pl.ds(k * LANES, LANES)] = b[k]

    def bwd(j, carry):
        a, b = carry
        i = steps - 1 - j
        g = gn_ref[i]
        new_a, new_b = [], []
        for k in range(chunks):
            e = jnp.exp(-(g * rs[k]))
            u = up_refs[k][pl.ds(i, segs, stride=steps), :]
            new_a.append(a[k] * e)
            new_b.append(e * b[k] + u)
        return (tuple(new_a), tuple(new_b))

    a, b = lax.fori_loop(0, steps, bwd, (ones, zeros), unroll=UNROLL)
    for k in range(chunks):
        ba_ref[:, pl.ds(k * LANES, LANES)] = a[k]
        bb_ref[:, pl.ds(k * LANES, LANES)] = b[k]


def _sweep_kernel(g_ref, gn_ref, r_ref, if_ref, ib_ref, *refs):
    chunks = (len(refs) - 2) // 2
    drive_refs = refs[:chunks]
    up_refs = refs[chunks:2 * chunks]
    st_ref, adj_ref = refs[2 * chunks:]
    steps, segs, _ = g_ref.shape
    rs = [r_ref[:, pl.ds(k * LANES, LANES)] for k in range(chunks)]

    def fwd(i, b):
        g = g_ref[i]
        out = []
        for k in range(chunks):
            d = jnp.exp(-(g * rs[k]))
            v = d * b[k] + drive_refs[k][pl.ds(i, segs, stride=steps), :]
            st_ref[k, pl.ds(i, segs, stride=steps), :] = v
            out.append(v)
        return tuple(out)

    init = tuple(if_ref[:, pl.ds(k * LANES, LANES)] for k in range(chunks))
    lax.fori_loop(0, steps, fwd, init, unroll=UNROLL)

    def bwd(j, b):
        i = steps - 1 - j
        g = gn_ref[i]
        out = []
        for k in range(chunks):
            e = jnp.exp(-(g * rs[k]))
            v = e * b[k] + up_refs[k][pl.ds(i, segs, stride=steps), :]
            adj_ref[k, pl.ds(i, segs, stride=steps), :] = v
            out.append(v)
        return tuple(out)

    init = tuple(ib_ref[:, pl.ds(k * LANES, LANES)] for k in range(chunks))
    lax.fori_loop(0, steps, bwd, init, unroll=UNROLL)


def _column_specs(total, width):
    return [pl.BlockSpec((total, LANES), lambda j, k=k: (0, k)) for k in range(width // LANES)]


def _whole(shape):
    return pl.BlockSpec(shape, lambda j: (0,) * len(shape))


def local_summaries(g3, gn3, rates2, drive, up):
    total, width = drive.shape
    steps, segs, _ = g3.shape
    chunks = width // LANES
    cols = _column_specs(total, width)
    seg_shape = jax.ShapeDtypeStruct((segs, width), jnp.float32)
    return pl.pallas_call(
        _summary_kernel,
        grid=(1,),
        in_specs=[_whole(g3.shape), _whole(gn3.shape), _whole(rates2.shape)] + cols + cols,
        out_specs=[_whole((segs, width))] * 4,
        out_shape=[seg_shape] * 4,
        compiler_params=pltpu.CompilerParams(vmem_limit_bytes=48 * 1024 * 1024),
    )(g3, gn3, rates2, *([drive] * chunks), *([up] * chunks))


def sweeps(g3, gn3, rates2, drive, up, init_f, init_b):
    total, width = drive.shape
    steps, segs, _ = g3.shape
    chunks = width // LANES
    cols = _column_specs(total, width)
    full = jax.ShapeDtypeStruct((chunks, total, LANES), jnp.float32)
    return pl.pallas_call(
        _sweep_kernel,
        grid=(1,),
        in_specs=[_whole(g3.shape), _whole(gn3.shape), _whole(rates2.shape),
                  _whole(init_f.shape), _whole(init_b.shape)] + cols + cols,
        out_specs=[_whole(full.shape)] * 2,
        out_shape=[full, full],
        compiler_params=pltpu.CompilerParams(vmem_limit_bytes=48 * 1024 * 1024),
    )(g3, gn3, rates2, init_f, init_b, *([drive] * chunks), *([up] * chunks))


def local(inputs, gaps, rates, w_in, w_out, cotangent):
    total = inputs.shape[0]
    width = rates.shape[0]
    segs = SEGMENTS
    steps = total // segs
    peers = lax.axis_size(SEQ)
    place = lax.axis_index(SEQ)
    factor = 1.0 / math.sqrt(total * peers)

    gain = jnp.sqrt(-jnp.expm1(-2.0 * gaps[:, None] * rates[None, :]))
    drive = gain * jnp.dot(inputs, w_in, preferred_element_type=jnp.float32)
    upstream = lax.dot_general(
        cotangent, w_out, (((1,), (1,)), ((), ())), preferred_element_type=jnp.float32
    )
    gaps_next = jnp.concatenate([gaps[1:], jnp.zeros((1,), jnp.float32)], 0)
    g3 = gaps.reshape(segs, steps).T[:, :, None]
    gn3 = gaps_next.reshape(segs, steps).T[:, :, None]
    rates2 = rates[None, :]

    fa, fb, ba, bb = local_summaries(g3, gn3, rates2, drive, up=upstream)

    end_state = jnp.zeros((width,), jnp.float32)
    block_decay = jnp.ones((width,), jnp.float32)
    for s in range(segs):
        end_state = fb[s] + fa[s] * end_state
        block_decay = block_decay * fa[s]
    first_adj = jnp.zeros((width,), jnp.float32)
    for s in reversed(range(segs)):
        first_adj = bb[s] + ba[s] * first_adj
    start_adj = jnp.exp(-gaps[0] * rates) * first_adj

    summary = jnp.stack([block_decay, end_state, start_adj], 0)
    gathered = lax.all_gather(lax.all_gather(summary, "sz"), "sx").reshape(peers, 3, width)
    carry_in = jnp.zeros((width,), jnp.float32)
    for q in range(peers):
        new = gathered[q, 1] + gathered[q, 0] * carry_in
        carry_in = jnp.where(q < place, new, carry_in)
    right_in = jnp.zeros((width,), jnp.float32)
    for q in reversed(range(peers)):
        new = gathered[q, 2] + gathered[q, 0] * right_in
        right_in = jnp.where(q > place, new, right_in)

    inits_f = []
    e = carry_in
    for s in range(segs):
        inits_f.append(e)
        e = fb[s] + fa[s] * e
    inits_b = [None] * segs
    v = right_in
    for s in reversed(range(segs)):
        inits_b[s] = v
        v = bb[s] + ba[s] * v
    init_f = jnp.stack(inits_f, 0)
    init_b = jnp.stack(inits_b, 0)

    state, adjoint = sweeps(g3, gn3, rates2, drive, upstream, init_f, init_b)
    chunks = width // LANES
    gain3 = gain.reshape(total, chunks, LANES).transpose(1, 0, 2)
    drive_grad = (gain3 * adjoint).astype(jnp.bfloat16)
    state_low = state.astype(jnp.bfloat16)
    in_term = lax.dot_general(
        inputs, drive_grad, (((0,), (1,)), ((), ())), preferred_element_type=jnp.float32
    ).reshape(inputs.shape[1], width) * factor
    out_term = lax.dot_general(
        cotangent, state_low, (((0,), (1,)), ((), ())), preferred_element_type=jnp.float32
    ).reshape(cotangent.shape[1], width) * factor
    joined = jnp.concatenate([in_term, out_term], 1).astype(jnp.bfloat16)
    joined = lax.psum_scatter(joined, "sx", scatter_dimension=0, tiled=True)
    joined = lax.psum_scatter(joined, "sz", scatter_dimension=0, tiled=True).astype(jnp.float32)
    d_w_in = joined[:, :width]
    d_w_out = joined[:, width:].T
    w_in3 = w_in.reshape(w_in.shape[0], chunks, LANES)
    partial_value = lax.dot_general(
        drive_grad, w_in3, (((0, 2), (1, 2)), ((), ())), preferred_element_type=jnp.float32
    )
    d_inputs = lax.psum_scatter(
        partial_value.astype(jnp.bfloat16), CHAN, scatter_dimension=1, tiled=True
    )
    return (d_inputs, d_w_in, d_w_out)


SEQ = ("sx", "sz")
CHAN = ("cy", "cc")


def solution(mesh):
    grid = mesh.devices
    seq_size, chan_size = grid.shape
    z_size = len({d.coords[2] for d in grid[:, 0]})
    core_size = len({d.core_on_chip for d in grid[0, :]})
    split = Mesh(
        grid.reshape(seq_size // z_size, z_size, chan_size // core_size, core_size),
        ("sx", "sz", "cy", "cc"),
    )
    placed = (P(SEQ, None), P(SEQ), P(CHAN), P(None, CHAN), P(CHAN, None), P(SEQ, None))
    return jax.shard_map(
        local,
        mesh=split,
        in_specs=placed,
        out_specs=(P(SEQ, CHAN), P(SEQ, CHAN), P(CHAN, SEQ)),
        check_vma=False,
    )
```

```python
import math

import jax
import jax.numpy as jnp
from jax import lax
from jax.experimental import pallas as pl
from jax.experimental.pallas import tpu as pltpu
from jax.sharding import Mesh, PartitionSpec as P

SEGMENTS = 16
LANES = 128
UNROLL = 8


def _summary_kernel(g_ref, gn_ref, r_ref, *refs):
    chunks = (len(refs) - 4) // 2
    drive_refs = refs[:chunks]
    up_refs = refs[chunks:2 * chunks]
    fa_ref, fb_ref, ba_ref, bb_ref = refs[2 * chunks:]
    steps, segs, _ = g_ref.shape
    rs = [r_ref[:, pl.ds(k * LANES, LANES)] for k in range(chunks)]
    ones = tuple(jnp.ones((segs, LANES), jnp.float32) for _ in range(chunks))
    zeros = tuple(jnp.zeros((segs, LANES), jnp.float32) for _ in range(chunks))

    def fwd(i, carry):
        a, b = carry
        g = g_ref[i]
        new_a, new_b = [], []
        for k in range(chunks):
            d = jnp.exp(-(g * rs[k]))
            x = drive_refs[k][pl.ds(i, segs, stride=steps), :]
            new_a.append(a[k] * d)
            new_b.append(d * b[k] + x)
        return (tuple(new_a), tuple(new_b))

    a, b = lax.fori_loop(0, steps, fwd, (ones, zeros), unroll=UNROLL)
    for k in range(chunks):
        fa_ref[:, pl.ds(k * LANES, LANES)] = a[k]
        fb_ref[:, pl.ds(k * LANES, LANES)] = b[k]

    def bwd(j, carry):
        a, b = carry
        i = steps - 1 - j
        g = gn_ref[i]
        new_a, new_b = [], []
        for k in range(chunks):
            e = jnp.exp(-(g * rs[k]))
            u = up_refs[k][pl.ds(i, segs, stride=steps), :]
            new_a.append(a[k] * e)
            new_b.append(e * b[k] + u)
        return (tuple(new_a), tuple(new_b))

    a, b = lax.fori_loop(0, steps, bwd, (ones, zeros), unroll=UNROLL)
    for k in range(chunks):
        ba_ref[:, pl.ds(k * LANES, LANES)] = a[k]
        bb_ref[:, pl.ds(k * LANES, LANES)] = b[k]


def _sweep_kernel(g_ref, gn_ref, r_ref, if_ref, ib_ref, *refs):
    chunks = (len(refs) - 2) // 2
    drive_refs = refs[:chunks]
    up_refs = refs[chunks:2 * chunks]
    st_ref, adj_ref = refs[2 * chunks:]
    steps, segs, _ = g_ref.shape
    rs = [r_ref[:, pl.ds(k * LANES, LANES)] for k in range(chunks)]

    def fwd(i, b):
        g = g_ref[i]
        out = []
        for k in range(chunks):
            d = jnp.exp(-(g * rs[k]))
            v = d * b[k] + drive_refs[k][pl.ds(i, segs, stride=steps), :]
            st_ref[k, pl.ds(i, segs, stride=steps), :] = v
            out.append(v)
        return tuple(out)

    init = tuple(if_ref[:, pl.ds(k * LANES, LANES)] for k in range(chunks))
    lax.fori_loop(0, steps, fwd, init, unroll=UNROLL)

    def bwd(j, b):
        i = steps - 1 - j
        g = gn_ref[i]
        out = []
        for k in range(chunks):
            e = jnp.exp(-(g * rs[k]))
            v = e * b[k] + up_refs[k][pl.ds(i, segs, stride=steps), :]
            adj_ref[k, pl.ds(i, segs, stride=steps), :] = v
            out.append(v)
        return tuple(out)

    init = tuple(ib_ref[:, pl.ds(k * LANES, LANES)] for k in range(chunks))
    lax.fori_loop(0, steps, bwd, init, unroll=UNROLL)


def _column_specs(total, width):
    return [pl.BlockSpec((total, LANES), lambda j, k=k: (0, k)) for k in range(width // LANES)]


def _whole(shape):
    return pl.BlockSpec(shape, lambda j: (0,) * len(shape))


def local_summaries(g3, gn3, rates2, drive, up):
    total, width = drive.shape
    steps, segs, _ = g3.shape
    chunks = width // LANES
    cols = _column_specs(total, width)
    seg_shape = jax.ShapeDtypeStruct((segs, width), jnp.float32)
    return pl.pallas_call(
        _summary_kernel,
        grid=(1,),
        in_specs=[_whole(g3.shape), _whole(gn3.shape), _whole(rates2.shape)] + cols + cols,
        out_specs=[_whole((segs, width))] * 4,
        out_shape=[seg_shape] * 4,
        compiler_params=pltpu.CompilerParams(vmem_limit_bytes=48 * 1024 * 1024),
    )(g3, gn3, rates2, *([drive] * chunks), *([up] * chunks))


def sweeps(g3, gn3, rates2, drive, up, init_f, init_b):
    total, width = drive.shape
    steps, segs, _ = g3.shape
    chunks = width // LANES
    cols = _column_specs(total, width)
    full = jax.ShapeDtypeStruct((chunks, total, LANES), jnp.float32)
    return pl.pallas_call(
        _sweep_kernel,
        grid=(1,),
        in_specs=[_whole(g3.shape), _whole(gn3.shape), _whole(rates2.shape),
                  _whole(init_f.shape), _whole(init_b.shape)] + cols + cols,
        out_specs=[_whole(full.shape)] * 2,
        out_shape=[full, full],
        compiler_params=pltpu.CompilerParams(vmem_limit_bytes=48 * 1024 * 1024),
    )(g3, gn3, rates2, init_f, init_b, *([drive] * chunks), *([up] * chunks))


def local(inputs, gaps, rates, w_in, w_out, cotangent):
    total = inputs.shape[0]
    width = rates.shape[0]
    segs = SEGMENTS
    steps = total // segs
    peers = lax.axis_size(SEQ)
    place = lax.axis_index(SEQ)
    factor = 1.0 / math.sqrt(total * peers)

    gain = jnp.sqrt(-jnp.expm1(-2.0 * gaps[:, None] * rates[None, :]))
    drive = gain * jnp.dot(inputs, w_in, preferred_element_type=jnp.float32)
    upstream = lax.dot_general(
        cotangent, w_out, (((1,), (1,)), ((), ())), preferred_element_type=jnp.float32
    )
    gaps_next = jnp.concatenate([gaps[1:], jnp.zeros((1,), jnp.float32)], 0)
    g3 = gaps.reshape(segs, steps).T[:, :, None]
    gn3 = gaps_next.reshape(segs, steps).T[:, :, None]
    rates2 = rates[None, :]

    fa, fb, ba, bb = local_summaries(g3, gn3, rates2, drive, up=upstream)

    end_state = jnp.zeros((width,), jnp.float32)
    block_decay = jnp.ones((width,), jnp.float32)
    for s in range(segs):
        end_state = fb[s] + fa[s] * end_state
        block_decay = block_decay * fa[s]
    first_adj = jnp.zeros((width,), jnp.float32)
    for s in reversed(range(segs)):
        first_adj = bb[s] + ba[s] * first_adj
    start_adj = jnp.exp(-gaps[0] * rates) * first_adj

    summary = jnp.stack([block_decay, end_state, start_adj], 0)
    gathered = lax.all_gather(lax.all_gather(summary, "sz"), "sx").reshape(peers, 3, width)
    carry_in = jnp.zeros((width,), jnp.float32)
    for q in range(peers):
        new = gathered[q, 1] + gathered[q, 0] * carry_in
        carry_in = jnp.where(q < place, new, carry_in)
    right_in = jnp.zeros((width,), jnp.float32)
    for q in reversed(range(peers)):
        new = gathered[q, 2] + gathered[q, 0] * right_in
        right_in = jnp.where(q > place, new, right_in)

    inits_f = []
    e = carry_in
    for s in range(segs):
        inits_f.append(e)
        e = fb[s] + fa[s] * e
    inits_b = [None] * segs
    v = right_in
    for s in reversed(range(segs)):
        inits_b[s] = v
        v = bb[s] + ba[s] * v
    init_f = jnp.stack(inits_f, 0)
    init_b = jnp.stack(inits_b, 0)

    state, adjoint = sweeps(g3, gn3, rates2, drive, upstream, init_f, init_b)
    chunks = width // LANES
    gain3 = gain.reshape(total, chunks, LANES).transpose(1, 0, 2)
    drive_grad = (gain3 * adjoint).astype(jnp.bfloat16)
    state_low = state.astype(jnp.bfloat16)
    in_term = lax.dot_general(
        inputs, drive_grad, (((0,), (1,)), ((), ())), preferred_element_type=jnp.float32
    ).reshape(inputs.shape[1], width) * factor
    out_term = lax.dot_general(
        cotangent, state_low, (((0,), (1,)), ((), ())), preferred_element_type=jnp.float32
    ).reshape(cotangent.shape[1], width) * factor
    joined = jnp.concatenate([in_term, out_term], 1).astype(jnp.bfloat16)
    joined = lax.psum_scatter(joined, "sx", scatter_dimension=0, tiled=True)
    joined = lax.psum_scatter(joined, "sz", scatter_dimension=0, tiled=True).astype(jnp.float32)
    d_w_in = joined[:, :width]
    d_w_out = joined[:, width:].T
    ys = lax.axis_size("cy")
    cores = lax.axis_size("cc")
    dmodel = w_in.shape[0]
    w_perm = (
        w_in.reshape(ys, cores, dmodel // (ys * cores), chunks, LANES)
        .transpose(1, 0, 2, 3, 4)
        .reshape(dmodel, chunks, LANES)
    )
    partial_t = lax.dot_general(
        w_perm, drive_grad, (((1, 2), (0, 2)), ((), ())), preferred_element_type=jnp.float32
    ).astype(jnp.bfloat16)
    partial_t = lax.psum_scatter(partial_t, "cc", scatter_dimension=0, tiled=True)
    d_inputs = lax.psum_scatter(partial_t, "cy", scatter_dimension=0, tiled=True).T
    return (d_inputs, d_w_in, d_w_out)


SEQ = ("sx", "sz")
CHAN = ("cy", "cc")


def solution(mesh):
    grid = mesh.devices
    seq_size, chan_size = grid.shape
    z_size = len({d.coords[2] for d in grid[:, 0]})
    core_size = len({d.core_on_chip for d in grid[0, :]})
    split = Mesh(
        grid.reshape(seq_size // z_size, z_size, chan_size // core_size, core_size),
        ("sx", "sz", "cy", "cc"),
    )
    placed = (P(SEQ, None), P(SEQ), P(CHAN), P(None, CHAN), P(CHAN, None), P(SEQ, None))
    return jax.shard_map(
        local,
        mesh=split,
        in_specs=placed,
        out_specs=(P(SEQ, CHAN), P(SEQ, CHAN), P(CHAN, SEQ)),
        check_vma=False,
    )
```

```python
import math

import jax
import jax.numpy as jnp
from jax import lax
from jax.experimental import pallas as pl
from jax.experimental.pallas import tpu as pltpu
from jax.sharding import Mesh, PartitionSpec as P

SEGMENTS = 8
LANES = 128
UNROLL = 8


def _summary_kernel(g_ref, gn_ref, r_ref, *refs):
    chunks = (len(refs) - 4) // 2
    drive_refs = refs[:chunks]
    up_refs = refs[chunks:2 * chunks]
    fa_ref, fb_ref, ba_ref, bb_ref = refs[2 * chunks:]
    steps, segs, _ = g_ref.shape
    rs = [r_ref[:, pl.ds(k * LANES, LANES)] for k in range(chunks)]
    ones = tuple(jnp.ones((segs, LANES), jnp.float32) for _ in range(chunks))
    zeros = tuple(jnp.zeros((segs, LANES), jnp.float32) for _ in range(chunks))

    def fwd(i, carry):
        a, b = carry
        g = g_ref[i]
        new_a, new_b = [], []
        for k in range(chunks):
            d = jnp.exp(-(g * rs[k]))
            x = drive_refs[k][pl.ds(i, segs, stride=steps), :]
            new_a.append(a[k] * d)
            new_b.append(d * b[k] + x)
        return (tuple(new_a), tuple(new_b))

    a, b = lax.fori_loop(0, steps, fwd, (ones, zeros), unroll=UNROLL)
    for k in range(chunks):
        fa_ref[:, pl.ds(k * LANES, LANES)] = a[k]
        fb_ref[:, pl.ds(k * LANES, LANES)] = b[k]

    def bwd(j, carry):
        a, b = carry
        i = steps - 1 - j
        g = gn_ref[i]
        new_a, new_b = [], []
        for k in range(chunks):
            e = jnp.exp(-(g * rs[k]))
            u = up_refs[k][pl.ds(i, segs, stride=steps), :]
            new_a.append(a[k] * e)
            new_b.append(e * b[k] + u)
        return (tuple(new_a), tuple(new_b))

    a, b = lax.fori_loop(0, steps, bwd, (ones, zeros), unroll=UNROLL)
    for k in range(chunks):
        ba_ref[:, pl.ds(k * LANES, LANES)] = a[k]
        bb_ref[:, pl.ds(k * LANES, LANES)] = b[k]


def _sweep_kernel(g_ref, gn_ref, r_ref, if_ref, ib_ref, *refs):
    chunks = (len(refs) - 2) // 2
    drive_refs = refs[:chunks]
    up_refs = refs[chunks:2 * chunks]
    st_ref, adj_ref = refs[2 * chunks:]
    steps, segs, _ = g_ref.shape
    rs = [r_ref[:, pl.ds(k * LANES, LANES)] for k in range(chunks)]

    def fwd(i, b):
        g = g_ref[i]
        out = []
        for k in range(chunks):
            d = jnp.exp(-(g * rs[k]))
            v = d * b[k] + drive_refs[k][pl.ds(i, segs, stride=steps), :]
            st_ref[k, pl.ds(i, segs, stride=steps), :] = v
            out.append(v)
        return tuple(out)

    init = tuple(if_ref[:, pl.ds(k * LANES, LANES)] for k in range(chunks))
    lax.fori_loop(0, steps, fwd, init, unroll=UNROLL)

    def bwd(j, b):
        i = steps - 1 - j
        g = gn_ref[i]
        out = []
        for k in range(chunks):
            e = jnp.exp(-(g * rs[k]))
            v = e * b[k] + up_refs[k][pl.ds(i, segs, stride=steps), :]
            adj_ref[k, pl.ds(i, segs, stride=steps), :] = v
            out.append(v)
        return tuple(out)

    init = tuple(ib_ref[:, pl.ds(k * LANES, LANES)] for k in range(chunks))
    lax.fori_loop(0, steps, bwd, init, unroll=UNROLL)


def _column_specs(total, width):
    return [pl.BlockSpec((total, LANES), lambda j, k=k: (0, k)) for k in range(width // LANES)]


def _whole(shape):
    return pl.BlockSpec(shape, lambda j: (0,) * len(shape))


def local_summaries(g3, gn3, rates2, drive, up):
    total, width = drive.shape
    steps, segs, _ = g3.shape
    chunks = width // LANES
    cols = _column_specs(total, width)
    seg_shape = jax.ShapeDtypeStruct((segs, width), jnp.float32)
    return pl.pallas_call(
        _summary_kernel,
        grid=(1,),
        in_specs=[_whole(g3.shape), _whole(gn3.shape), _whole(rates2.shape)] + cols + cols,
        out_specs=[_whole((segs, width))] * 4,
        out_shape=[seg_shape] * 4,
        compiler_params=pltpu.CompilerParams(vmem_limit_bytes=48 * 1024 * 1024),
    )(g3, gn3, rates2, *([drive] * chunks), *([up] * chunks))


def sweeps(g3, gn3, rates2, drive, up, init_f, init_b):
    total, width = drive.shape
    steps, segs, _ = g3.shape
    chunks = width // LANES
    cols = _column_specs(total, width)
    full = jax.ShapeDtypeStruct((chunks, total, LANES), jnp.float32)
    return pl.pallas_call(
        _sweep_kernel,
        grid=(1,),
        in_specs=[_whole(g3.shape), _whole(gn3.shape), _whole(rates2.shape),
                  _whole(init_f.shape), _whole(init_b.shape)] + cols + cols,
        out_specs=[_whole(full.shape)] * 2,
        out_shape=[full, full],
        compiler_params=pltpu.CompilerParams(vmem_limit_bytes=48 * 1024 * 1024),
    )(g3, gn3, rates2, init_f, init_b, *([drive] * chunks), *([up] * chunks))


def _pick(x, index):
    return lax.dynamic_index_in_dim(x, index, 0, keepdims=False)


def chan_reduce(partial_t):
    ys = lax.axis_size("cy")
    cores = lax.axis_size("cc")
    y = lax.axis_index("cy")
    core = lax.axis_index("cc")
    dmodel, total = partial_t.shape
    blk = dmodel // (ys * cores)
    parts = partial_t.reshape(ys, cores, blk, total).transpose(1, 0, 2, 3)
    mine = _pick(parts, core).astype(jnp.float32)
    other = _pick(parts, (core + 1) % cores)
    swap = [(i, (i + 1) % cores) for i in range(cores)]
    acc = mine + lax.ppermute(other, "cc", swap).astype(jnp.float32)
    half = total // 2
    ahead = acc[:, :, :half]
    behind = acc[:, :, half:]
    up_ring = [(i, (i + 1) % ys) for i in range(ys)]
    down_ring = [(i, (i - 1) % ys) for i in range(ys)]
    buf_a = _pick(ahead, (y - 1) % ys)
    buf_b = _pick(behind, (y + 1) % ys)
    for k in range(ys - 1):
        got_a = lax.ppermute(buf_a.astype(jnp.bfloat16), "cy", up_ring)
        got_b = lax.ppermute(buf_b.astype(jnp.bfloat16), "cy", down_ring)
        buf_a = _pick(ahead, (y - k - 2) % ys) + got_a.astype(jnp.float32)
        buf_b = _pick(behind, (y + k + 2) % ys) + got_b.astype(jnp.float32)
    return jnp.concatenate([buf_a, buf_b], 1).astype(jnp.bfloat16)


def local(inputs, gaps, rates, w_in, w_out, cotangent):
    total = inputs.shape[0]
    width = rates.shape[0]
    segs = SEGMENTS
    steps = total // segs
    peers = lax.axis_size(SEQ)
    place = lax.axis_index(SEQ)
    factor = 1.0 / math.sqrt(total * peers)

    gain = jnp.sqrt(-jnp.expm1(-2.0 * gaps[:, None] * rates[None, :]))
    drive = gain * jnp.dot(inputs, w_in, preferred_element_type=jnp.float32)
    upstream = lax.dot_general(
        cotangent, w_out, (((1,), (1,)), ((), ())), preferred_element_type=jnp.float32
    )
    gaps_next = jnp.concatenate([gaps[1:], jnp.zeros((1,), jnp.float32)], 0)
    g3 = gaps.reshape(segs, steps).T[:, :, None]
    gn3 = gaps_next.reshape(segs, steps).T[:, :, None]
    rates2 = rates[None, :]

    fa, fb, ba, bb = local_summaries(g3, gn3, rates2, drive, up=upstream)

    end_state = jnp.zeros((width,), jnp.float32)
    block_decay = jnp.ones((width,), jnp.float32)
    for s in range(segs):
        end_state = fb[s] + fa[s] * end_state
        block_decay = block_decay * fa[s]
    first_adj = jnp.zeros((width,), jnp.float32)
    for s in reversed(range(segs)):
        first_adj = bb[s] + ba[s] * first_adj
    start_adj = jnp.exp(-gaps[0] * rates) * first_adj

    summary = jnp.stack([block_decay, end_state, start_adj], 0)
    gathered = lax.all_gather(lax.all_gather(summary, "sz"), "sx").reshape(peers, 3, width)
    carry_in = jnp.zeros((width,), jnp.float32)
    for q in range(peers):
        new = gathered[q, 1] + gathered[q, 0] * carry_in
        carry_in = jnp.where(q < place, new, carry_in)
    right_in = jnp.zeros((width,), jnp.float32)
    for q in reversed(range(peers)):
        new = gathered[q, 2] + gathered[q, 0] * right_in
        right_in = jnp.where(q > place, new, right_in)

    inits_f = []
    e = carry_in
    for s in range(segs):
        inits_f.append(e)
        e = fb[s] + fa[s] * e
    inits_b = [None] * segs
    v = right_in
    for s in reversed(range(segs)):
        inits_b[s] = v
        v = bb[s] + ba[s] * v
    init_f = jnp.stack(inits_f, 0)
    init_b = jnp.stack(inits_b, 0)

    state, adjoint = sweeps(g3, gn3, rates2, drive, upstream, init_f, init_b)
    chunks = width // LANES
    gain3 = gain.reshape(total, chunks, LANES).transpose(1, 0, 2)
    drive_grad = (gain3 * adjoint).astype(jnp.bfloat16)
    state_low = state.astype(jnp.bfloat16)
    in_term = lax.dot_general(
        inputs, drive_grad, (((0,), (1,)), ((), ())), preferred_element_type=jnp.float32
    ).reshape(inputs.shape[1], width) * factor
    out_term = lax.dot_general(
        cotangent, state_low, (((0,), (1,)), ((), ())), preferred_element_type=jnp.float32
    ).reshape(cotangent.shape[1], width) * factor
    joined = jnp.concatenate([in_term, out_term], 1).astype(jnp.bfloat16)
    joined = lax.psum_scatter(joined, "sx", scatter_dimension=0, tiled=True)
    joined = lax.psum_scatter(joined, "sz", scatter_dimension=0, tiled=True).astype(jnp.float32)
    d_w_in = joined[:, :width]
    d_w_out = joined[:, width:].T
    w_in3 = w_in.reshape(w_in.shape[0], chunks, LANES)
    partial_t = lax.dot_general(
        w_in3, drive_grad, (((1, 2), (0, 2)), ((), ())), preferred_element_type=jnp.float32
    ).astype(jnp.bfloat16)
    d_inputs = chan_reduce(partial_t).T
    return (d_inputs, d_w_in, d_w_out)


SEQ = ("sx", "sz")
CHAN = ("cy", "cc")


def solution(mesh):
    grid = mesh.devices
    seq_size, chan_size = grid.shape
    z_size = len({d.coords[2] for d in grid[:, 0]})
    core_size = len({d.core_on_chip for d in grid[0, :]})
    split = Mesh(
        grid.reshape(seq_size // z_size, z_size, chan_size // core_size, core_size),
        ("sx", "sz", "cy", "cc"),
    )
    placed = (P(SEQ, None), P(SEQ), P(CHAN), P(None, CHAN), P(CHAN, None), P(SEQ, None))
    return jax.shard_map(
        local,
        mesh=split,
        in_specs=placed,
        out_specs=(P(SEQ, CHAN), P(SEQ, CHAN), P(CHAN, SEQ)),
        check_vma=False,
    )
```

```python
import math

import jax
import jax.numpy as jnp
from jax import lax
from jax.experimental import pallas as pl
from jax.experimental.pallas import tpu as pltpu
from jax.sharding import Mesh, PartitionSpec as P

SEGMENTS = 8
LANES = 128
UNROLL = 8


def _summary_kernel(g_ref, gn_ref, r_ref, *refs):
    chunks = (len(refs) - 4) // 2
    drive_refs = refs[:chunks]
    up_refs = refs[chunks:2 * chunks]
    fa_ref, fb_ref, ba_ref, bb_ref = refs[2 * chunks:]
    steps, segs, _ = g_ref.shape
    rs = [r_ref[:, pl.ds(k * LANES, LANES)] for k in range(chunks)]
    ones = tuple(jnp.ones((segs, LANES), jnp.float32) for _ in range(chunks))
    zeros = tuple(jnp.zeros((segs, LANES), jnp.float32) for _ in range(chunks))

    def fwd(i, carry):
        a, b = carry
        g = g_ref[i]
        new_a, new_b = [], []
        for k in range(chunks):
            d = jnp.exp(-(g * rs[k]))
            x = drive_refs[k][pl.ds(i, segs, stride=steps), :]
            new_a.append(a[k] * d)
            new_b.append(d * b[k] + x)
        return (tuple(new_a), tuple(new_b))

    a, b = lax.fori_loop(0, steps, fwd, (ones, zeros), unroll=UNROLL)
    for k in range(chunks):
        fa_ref[:, pl.ds(k * LANES, LANES)] = a[k]
        fb_ref[:, pl.ds(k * LANES, LANES)] = b[k]

    def bwd(j, carry):
        a, b = carry
        i = steps - 1 - j
        g = gn_ref[i]
        new_a, new_b = [], []
        for k in range(chunks):
            e = jnp.exp(-(g * rs[k]))
            u = up_refs[k][pl.ds(i, segs, stride=steps), :]
            new_a.append(a[k] * e)
            new_b.append(e * b[k] + u)
        return (tuple(new_a), tuple(new_b))

    a, b = lax.fori_loop(0, steps, bwd, (ones, zeros), unroll=UNROLL)
    for k in range(chunks):
        ba_ref[:, pl.ds(k * LANES, LANES)] = a[k]
        bb_ref[:, pl.ds(k * LANES, LANES)] = b[k]


def _sweep_kernel(g_ref, gn_ref, r_ref, if_ref, ib_ref, *refs):
    chunks = (len(refs) - 2) // 2
    drive_refs = refs[:chunks]
    up_refs = refs[chunks:2 * chunks]
    st_ref, adj_ref = refs[2 * chunks:]
    steps, segs, _ = g_ref.shape
    rs = [r_ref[:, pl.ds(k * LANES, LANES)] for k in range(chunks)]

    def fwd(i, b):
        g = g_ref[i]
        out = []
        for k in range(chunks):
            d = jnp.exp(-(g * rs[k]))
            v = d * b[k] + drive_refs[k][pl.ds(i, segs, stride=steps), :]
            st_ref[k, pl.ds(i, segs, stride=steps), :] = v
            out.append(v)
        return tuple(out)

    init = tuple(if_ref[:, pl.ds(k * LANES, LANES)] for k in range(chunks))
    lax.fori_loop(0, steps, fwd, init, unroll=UNROLL)

    def bwd(j, b):
        i = steps - 1 - j
        g = gn_ref[i]
        out = []
        for k in range(chunks):
            e = jnp.exp(-(g * rs[k]))
            v = e * b[k] + up_refs[k][pl.ds(i, segs, stride=steps), :]
            adj_ref[k, pl.ds(i, segs, stride=steps), :] = v
            out.append(v)
        return tuple(out)

    init = tuple(ib_ref[:, pl.ds(k * LANES, LANES)] for k in range(chunks))
    lax.fori_loop(0, steps, bwd, init, unroll=UNROLL)


def _column_specs(total, width):
    return [pl.BlockSpec((total, LANES), lambda j, k=k: (0, k)) for k in range(width // LANES)]


def _whole(shape):
    return pl.BlockSpec(shape, lambda j: (0,) * len(shape))


def local_summaries(g3, gn3, rates2, drive, up):
    total, width = drive.shape
    steps, segs, _ = g3.shape
    chunks = width // LANES
    cols = _column_specs(total, width)
    seg_shape = jax.ShapeDtypeStruct((segs, width), jnp.float32)
    return pl.pallas_call(
        _summary_kernel,
        grid=(1,),
        in_specs=[_whole(g3.shape), _whole(gn3.shape), _whole(rates2.shape)] + cols + cols,
        out_specs=[_whole((segs, width))] * 4,
        out_shape=[seg_shape] * 4,
        compiler_params=pltpu.CompilerParams(vmem_limit_bytes=48 * 1024 * 1024),
    )(g3, gn3, rates2, *([drive] * chunks), *([up] * chunks))


def sweeps(g3, gn3, rates2, drive, up, init_f, init_b):
    total, width = drive.shape
    steps, segs, _ = g3.shape
    chunks = width // LANES
    cols = _column_specs(total, width)
    full = jax.ShapeDtypeStruct((chunks, total, LANES), jnp.float32)
    return pl.pallas_call(
        _sweep_kernel,
        grid=(1,),
        in_specs=[_whole(g3.shape), _whole(gn3.shape), _whole(rates2.shape),
                  _whole(init_f.shape), _whole(init_b.shape)] + cols + cols,
        out_specs=[_whole(full.shape)] * 2,
        out_shape=[full, full],
        compiler_params=pltpu.CompilerParams(vmem_limit_bytes=48 * 1024 * 1024),
    )(g3, gn3, rates2, init_f, init_b, *([drive] * chunks), *([up] * chunks))


def _pick(x, index, axis=0):
    return lax.dynamic_index_in_dim(x, index, axis, keepdims=False)


def chan_reduce(w_in, drive_grad):
    ys = lax.axis_size("cy")
    cores = lax.axis_size("cc")
    y = lax.axis_index("cy")
    core = lax.axis_index("cc")
    dmodel, width = w_in.shape
    chunks, total, lanes = drive_grad.shape
    blk = dmodel // (ys * cores)
    w_parts = w_in.reshape(ys, cores, blk, chunks, lanes)

    def product(index):
        rows = _pick(w_parts, index, 1)
        return jnp.stack([
            lax.dot_general(
                drive_grad, rows[j], (((0, 2), (1, 2)), ((), ())),
                preferred_element_type=jnp.float32,
            ).astype(jnp.bfloat16)
            for j in range(ys)
        ], 0)

    other = product((core + 1) % cores)
    swap = [(i, (i + 1) % cores) for i in range(cores)]
    got = lax.ppermute(other, "cc", swap)
    kept = product(core)
    half = total // 2

    def own(index, rows):
        return (_pick(kept, index)[rows].astype(jnp.float32)
                + _pick(got, index)[rows].astype(jnp.float32))

    first = slice(0, half)
    second = slice(half, total)
    up_ring = [(i, (i + 1) % ys) for i in range(ys)]
    down_ring = [(i, (i - 1) % ys) for i in range(ys)]
    buf_a = own((y - 1) % ys, first)
    buf_b = own((y + 1) % ys, second)
    for k in range(ys - 1):
        got_a = lax.ppermute(buf_a.astype(jnp.bfloat16), "cy", up_ring)
        got_b = lax.ppermute(buf_b.astype(jnp.bfloat16), "cy", down_ring)
        buf_a = own((y - k - 2) % ys, first) + got_a.astype(jnp.float32)
        buf_b = own((y + k + 2) % ys, second) + got_b.astype(jnp.float32)
    return jnp.concatenate([buf_a, buf_b], 0).astype(jnp.bfloat16)


def local(inputs, gaps, rates, w_in, w_out, cotangent):
    total = inputs.shape[0]
    width = rates.shape[0]
    segs = SEGMENTS
    steps = total // segs
    peers = lax.axis_size(SEQ)
    place = lax.axis_index(SEQ)
    factor = 1.0 / math.sqrt(total * peers)

    gain = jnp.sqrt(-jnp.expm1(-2.0 * gaps[:, None] * rates[None, :]))
    drive = gain * jnp.dot(inputs, w_in, preferred_element_type=jnp.float32)
    upstream = lax.dot_general(
        cotangent, w_out, (((1,), (1,)), ((), ())), preferred_element_type=jnp.float32
    )
    gaps_next = jnp.concatenate([gaps[1:], jnp.zeros((1,), jnp.float32)], 0)
    g3 = gaps.reshape(segs, steps).T[:, :, None]
    gn3 = gaps_next.reshape(segs, steps).T[:, :, None]
    rates2 = rates[None, :]

    fa, fb, ba, bb = local_summaries(g3, gn3, rates2, drive, up=upstream)

    end_state = jnp.zeros((width,), jnp.float32)
    block_decay = jnp.ones((width,), jnp.float32)
    for s in range(segs):
        end_state = fb[s] + fa[s] * end_state
        block_decay = block_decay * fa[s]
    first_adj = jnp.zeros((width,), jnp.float32)
    for s in reversed(range(segs)):
        first_adj = bb[s] + ba[s] * first_adj
    start_adj = jnp.exp(-gaps[0] * rates) * first_adj

    summary = jnp.stack([block_decay, end_state, start_adj], 0)
    gathered = lax.all_gather(lax.all_gather(summary, "sz"), "sx").reshape(peers, 3, width)
    carry_in = jnp.zeros((width,), jnp.float32)
    for q in range(peers):
        new = gathered[q, 1] + gathered[q, 0] * carry_in
        carry_in = jnp.where(q < place, new, carry_in)
    right_in = jnp.zeros((width,), jnp.float32)
    for q in reversed(range(peers)):
        new = gathered[q, 2] + gathered[q, 0] * right_in
        right_in = jnp.where(q > place, new, right_in)

    inits_f = []
    e = carry_in
    for s in range(segs):
        inits_f.append(e)
        e = fb[s] + fa[s] * e
    inits_b = [None] * segs
    v = right_in
    for s in reversed(range(segs)):
        inits_b[s] = v
        v = bb[s] + ba[s] * v
    init_f = jnp.stack(inits_f, 0)
    init_b = jnp.stack(inits_b, 0)

    state, adjoint = sweeps(g3, gn3, rates2, drive, upstream, init_f, init_b)
    chunks = width // LANES
    gain3 = gain.reshape(total, chunks, LANES).transpose(1, 0, 2)
    drive_grad = (gain3 * adjoint).astype(jnp.bfloat16)
    state_low = state.astype(jnp.bfloat16)
    in_term = lax.dot_general(
        inputs, drive_grad, (((0,), (1,)), ((), ())), preferred_element_type=jnp.float32
    ).reshape(inputs.shape[1], width) * factor
    out_term = lax.dot_general(
        cotangent, state_low, (((0,), (1,)), ((), ())), preferred_element_type=jnp.float32
    ).reshape(cotangent.shape[1], width) * factor
    joined = jnp.concatenate([in_term, out_term], 1).astype(jnp.bfloat16)
    joined = lax.psum_scatter(joined, "sx", scatter_dimension=0, tiled=True)
    joined = lax.psum_scatter(joined, "sz", scatter_dimension=0, tiled=True).astype(jnp.float32)
    d_w_in = joined[:, :width]
    d_w_out = joined[:, width:].T
    d_inputs = chan_reduce(w_in, drive_grad)
    return (d_inputs, d_w_in, d_w_out)


SEQ = ("sx", "sz")
CHAN = ("cy", "cc")


def solution(mesh):
    grid = mesh.devices
    seq_size, chan_size = grid.shape
    z_size = len({d.coords[2] for d in grid[:, 0]})
    core_size = len({d.core_on_chip for d in grid[0, :]})
    split = Mesh(
        grid.reshape(seq_size // z_size, z_size, chan_size // core_size, core_size),
        ("sx", "sz", "cy", "cc"),
    )
    placed = (P(SEQ, None), P(SEQ), P(CHAN), P(None, CHAN), P(CHAN, None), P(SEQ, None))
    return jax.shard_map(
        local,
        mesh=split,
        in_specs=placed,
        out_specs=(P(SEQ, CHAN), P(SEQ, CHAN), P(CHAN, SEQ)),
        check_vma=False,
    )
```

```python
import math

import jax
import jax.numpy as jnp
from jax import lax
from jax.experimental import pallas as pl
from jax.experimental.pallas import tpu as pltpu
from jax.sharding import Mesh, PartitionSpec as P

SEGMENTS = 8
LANES = 128
UNROLL = 8


def _summary_kernel(g_ref, gn_ref, r_ref, *refs):
    chunks = (len(refs) - 4) // 2
    drive_refs = refs[:chunks]
    up_refs = refs[chunks:2 * chunks]
    fa_ref, fb_ref, ba_ref, bb_ref = refs[2 * chunks:]
    steps, segs, _ = g_ref.shape
    rs = [r_ref[:, pl.ds(k * LANES, LANES)] for k in range(chunks)]
    ones = tuple(jnp.ones((segs, LANES), jnp.float32) for _ in range(chunks))
    zeros = tuple(jnp.zeros((segs, LANES), jnp.float32) for _ in range(chunks))

    def fwd(i, carry):
        a, b = carry
        g = g_ref[i]
        new_a, new_b = [], []
        for k in range(chunks):
            d = jnp.exp(-(g * rs[k]))
            x = drive_refs[k][pl.ds(i, segs, stride=steps), :]
            new_a.append(a[k] * d)
            new_b.append(d * b[k] + x)
        return (tuple(new_a), tuple(new_b))

    a, b = lax.fori_loop(0, steps, fwd, (ones, zeros), unroll=UNROLL)
    for k in range(chunks):
        fa_ref[:, pl.ds(k * LANES, LANES)] = a[k]
        fb_ref[:, pl.ds(k * LANES, LANES)] = b[k]

    def bwd(j, carry):
        a, b = carry
        i = steps - 1 - j
        g = gn_ref[i]
        new_a, new_b = [], []
        for k in range(chunks):
            e = jnp.exp(-(g * rs[k]))
            u = up_refs[k][pl.ds(i, segs, stride=steps), :]
            new_a.append(a[k] * e)
            new_b.append(e * b[k] + u)
        return (tuple(new_a), tuple(new_b))

    a, b = lax.fori_loop(0, steps, bwd, (ones, zeros), unroll=UNROLL)
    for k in range(chunks):
        ba_ref[:, pl.ds(k * LANES, LANES)] = a[k]
        bb_ref[:, pl.ds(k * LANES, LANES)] = b[k]


def _sweep_kernel(g_ref, gn_ref, r_ref, if_ref, ib_ref, *refs):
    chunks = (len(refs) - 2) // 2
    drive_refs = refs[:chunks]
    up_refs = refs[chunks:2 * chunks]
    st_ref, adj_ref = refs[2 * chunks:]
    steps, segs, _ = g_ref.shape
    rs = [r_ref[:, pl.ds(k * LANES, LANES)] for k in range(chunks)]

    def fwd(i, b):
        g = g_ref[i]
        out = []
        for k in range(chunks):
            d = jnp.exp(-(g * rs[k]))
            v = d * b[k] + drive_refs[k][pl.ds(i, segs, stride=steps), :]
            st_ref[k, pl.ds(i, segs, stride=steps), :] = v
            out.append(v)
        return tuple(out)

    init = tuple(if_ref[:, pl.ds(k * LANES, LANES)] for k in range(chunks))
    lax.fori_loop(0, steps, fwd, init, unroll=UNROLL)

    def bwd(j, b):
        i = steps - 1 - j
        g = gn_ref[i]
        out = []
        for k in range(chunks):
            e = jnp.exp(-(g * rs[k]))
            v = e * b[k] + up_refs[k][pl.ds(i, segs, stride=steps), :]
            adj_ref[k, pl.ds(i, segs, stride=steps), :] = v
            out.append(v)
        return tuple(out)

    init = tuple(ib_ref[:, pl.ds(k * LANES, LANES)] for k in range(chunks))
    lax.fori_loop(0, steps, bwd, init, unroll=UNROLL)


def _column_specs(total, width):
    return [pl.BlockSpec((total, LANES), lambda j, k=k: (0, k)) for k in range(width // LANES)]


def _whole(shape):
    return pl.BlockSpec(shape, lambda j: (0,) * len(shape))


def local_summaries(g3, gn3, rates2, drive, up):
    total, width = drive.shape
    steps, segs, _ = g3.shape
    chunks = width // LANES
    cols = _column_specs(total, width)
    seg_shape = jax.ShapeDtypeStruct((segs, width), jnp.float32)
    return pl.pallas_call(
        _summary_kernel,
        grid=(1,),
        in_specs=[_whole(g3.shape), _whole(gn3.shape), _whole(rates2.shape)] + cols + cols,
        out_specs=[_whole((segs, width))] * 4,
        out_shape=[seg_shape] * 4,
        compiler_params=pltpu.CompilerParams(vmem_limit_bytes=48 * 1024 * 1024),
    )(g3, gn3, rates2, *([drive] * chunks), *([up] * chunks))


def sweeps(g3, gn3, rates2, drive, up, init_f, init_b):
    total, width = drive.shape
    steps, segs, _ = g3.shape
    chunks = width // LANES
    cols = _column_specs(total, width)
    full = jax.ShapeDtypeStruct((chunks, total, LANES), jnp.float32)
    return pl.pallas_call(
        _sweep_kernel,
        grid=(1,),
        in_specs=[_whole(g3.shape), _whole(gn3.shape), _whole(rates2.shape),
                  _whole(init_f.shape), _whole(init_b.shape)] + cols + cols,
        out_specs=[_whole(full.shape)] * 2,
        out_shape=[full, full],
        compiler_params=pltpu.CompilerParams(vmem_limit_bytes=48 * 1024 * 1024),
    )(g3, gn3, rates2, init_f, init_b, *([drive] * chunks), *([up] * chunks))


def _pick(x, index):
    return lax.dynamic_index_in_dim(x, index, 0, keepdims=False)


def chan_reduce(partial_t):
    ys = lax.axis_size("cy")
    cores = lax.axis_size("cc")
    y = lax.axis_index("cy")
    core = lax.axis_index("cc")
    dmodel, total = partial_t.shape
    blk = dmodel // (ys * cores)
    parts = partial_t.reshape(ys, cores, blk, total).transpose(1, 0, 2, 3)
    mine = _pick(parts, core).astype(jnp.float32)
    other = _pick(parts, (core + 1) % cores)
    swap = [(i, (i + 1) % cores) for i in range(cores)]
    acc = mine + lax.ppermute(other, "cc", swap).astype(jnp.float32)
    half = total // 2
    ahead = acc[:, :, :half]
    behind = acc[:, :, half:]
    up_ring = [(i, (i + 1) % ys) for i in range(ys)]
    down_ring = [(i, (i - 1) % ys) for i in range(ys)]
    buf_a = _pick(ahead, (y - 1) % ys)
    buf_b = _pick(behind, (y + 1) % ys)
    for k in range(ys - 1):
        got_a = lax.ppermute(buf_a.astype(jnp.bfloat16), "cy", up_ring)
        got_b = lax.ppermute(buf_b.astype(jnp.bfloat16), "cy", down_ring)
        buf_a = _pick(ahead, (y - k - 2) % ys) + got_a.astype(jnp.float32)
        buf_b = _pick(behind, (y + k + 2) % ys) + got_b.astype(jnp.float32)
    return jnp.concatenate([buf_a, buf_b], 1).astype(jnp.bfloat16)


def local(inputs, gaps, rates, w_in, w_out, cotangent):
    total = inputs.shape[0]
    width = rates.shape[0]
    segs = SEGMENTS
    steps = total // segs
    peers = lax.axis_size(SEQ)
    place = lax.axis_index(SEQ)
    factor = 1.0 / math.sqrt(total * peers)

    gain = jnp.sqrt(-jnp.expm1(-2.0 * gaps[:, None] * rates[None, :]))
    drive = gain * jnp.dot(inputs, w_in, preferred_element_type=jnp.float32)
    upstream = lax.dot_general(
        cotangent, w_out, (((1,), (1,)), ((), ())), preferred_element_type=jnp.float32
    )
    gaps_next = jnp.concatenate([gaps[1:], jnp.zeros((1,), jnp.float32)], 0)
    g3 = gaps.reshape(segs, steps).T[:, :, None]
    gn3 = gaps_next.reshape(segs, steps).T[:, :, None]
    rates2 = rates[None, :]

    fa, fb, ba, bb = local_summaries(g3, gn3, rates2, drive, up=upstream)

    end_state = jnp.zeros((width,), jnp.float32)
    block_decay = jnp.ones((width,), jnp.float32)
    for s in range(segs):
        end_state = fb[s] + fa[s] * end_state
        block_decay = block_decay * fa[s]
    first_adj = jnp.zeros((width,), jnp.float32)
    for s in reversed(range(segs)):
        first_adj = bb[s] + ba[s] * first_adj
    start_adj = jnp.exp(-gaps[0] * rates) * first_adj

    summary = jnp.stack([block_decay, end_state, start_adj], 0)
    rel = [summary] + [
        lax.ppermute(summary, SEQ, [(i, (i + d) % peers) for i in range(peers)])
        for d in range(1, peers)
    ]
    carry_in = jnp.zeros((width,), jnp.float32)
    for d in reversed(range(1, peers)):
        new = rel[d][1] + rel[d][0] * carry_in
        carry_in = jnp.where(d <= place, new, carry_in)
    right_in = jnp.zeros((width,), jnp.float32)
    for d in range(1, peers):
        new = rel[d][2] + rel[d][0] * right_in
        right_in = jnp.where(d > place, new, right_in)

    inits_f = []
    e = carry_in
    for s in range(segs):
        inits_f.append(e)
        e = fb[s] + fa[s] * e
    inits_b = [None] * segs
    v = right_in
    for s in reversed(range(segs)):
        inits_b[s] = v
        v = bb[s] + ba[s] * v
    init_f = jnp.stack(inits_f, 0)
    init_b = jnp.stack(inits_b, 0)

    state, adjoint = sweeps(g3, gn3, rates2, drive, upstream, init_f, init_b)
    chunks = width // LANES
    gain3 = gain.reshape(total, chunks, LANES).transpose(1, 0, 2)
    drive_grad = (gain3 * adjoint).astype(jnp.bfloat16)
    state_low = state.astype(jnp.bfloat16)
    in_term = lax.dot_general(
        inputs, drive_grad, (((0,), (1,)), ((), ())), preferred_element_type=jnp.float32
    ).reshape(inputs.shape[1], width) * factor
    out_term = lax.dot_general(
        cotangent, state_low, (((0,), (1,)), ((), ())), preferred_element_type=jnp.float32
    ).reshape(cotangent.shape[1], width) * factor
    joined = jnp.concatenate([in_term, out_term], 1).astype(jnp.bfloat16)
    joined = lax.psum_scatter(joined, "sx", scatter_dimension=0, tiled=True)
    joined = lax.psum_scatter(joined, "sz", scatter_dimension=0, tiled=True).astype(jnp.float32)
    d_w_in = joined[:, :width]
    d_w_out = joined[:, width:].T
    w_in3 = w_in.reshape(w_in.shape[0], chunks, LANES)
    partial_t = lax.dot_general(
        w_in3, drive_grad, (((1, 2), (0, 2)), ((), ())), preferred_element_type=jnp.float32
    ).astype(jnp.bfloat16)
    d_inputs = chan_reduce(partial_t).T
    return (d_inputs, d_w_in, d_w_out)


SEQ = ("sx", "sz")
CHAN = ("cy", "cc")


def solution(mesh):
    grid = mesh.devices
    seq_size, chan_size = grid.shape
    z_size = len({d.coords[2] for d in grid[:, 0]})
    core_size = len({d.core_on_chip for d in grid[0, :]})
    split = Mesh(
        grid.reshape(seq_size // z_size, z_size, chan_size // core_size, core_size),
        ("sx", "sz", "cy", "cc"),
    )
    placed = (P(SEQ, None), P(SEQ), P(CHAN), P(None, CHAN), P(CHAN, None), P(SEQ, None))
    return jax.shard_map(
        local,
        mesh=split,
        in_specs=placed,
        out_specs=(P(SEQ, CHAN), P(SEQ, CHAN), P(CHAN, SEQ)),
        check_vma=False,
    )
```

```python
import math

import jax
import jax.numpy as jnp
from jax import lax
from jax.experimental import pallas as pl
from jax.experimental.pallas import tpu as pltpu
from jax.sharding import Mesh, PartitionSpec as P

SEGMENTS = 16
LANES = 128
UNROLL = 8


def _summary_kernel(g_ref, gn_ref, r_ref, drive_ref, up_ref, fa_ref, fb_ref, ba_ref, bb_ref):
    steps, segs, _ = g_ref.shape
    r = r_ref[...]
    ones = jnp.ones((segs, LANES), jnp.float32)
    zeros = jnp.zeros((segs, LANES), jnp.float32)

    def fwd(i, carry):
        a, b = carry
        d = jnp.exp(-(g_ref[i] * r))
        x = drive_ref[pl.ds(i, segs, stride=steps), :]
        return (a * d, d * b + x)

    a, b = lax.fori_loop(0, steps, fwd, (ones, zeros), unroll=UNROLL)
    fa_ref[...] = a
    fb_ref[...] = b

    def bwd(j, carry):
        a, b = carry
        i = steps - 1 - j
        e = jnp.exp(-(gn_ref[i] * r))
        u = up_ref[pl.ds(i, segs, stride=steps), :]
        return (a * e, e * b + u)

    a, b = lax.fori_loop(0, steps, bwd, (ones, zeros), unroll=UNROLL)
    ba_ref[...] = a
    bb_ref[...] = b


def _sweep_kernel(g_ref, gn_ref, r_ref, if_ref, ib_ref, drive_ref, up_ref, st_ref, adj_ref):
    steps, segs, _ = g_ref.shape
    r = r_ref[...]

    def fwd(i, b):
        d = jnp.exp(-(g_ref[i] * r))
        b = d * b + drive_ref[pl.ds(i, segs, stride=steps), :]
        st_ref[0, pl.ds(i, segs, stride=steps), :] = b
        return b

    lax.fori_loop(0, steps, fwd, if_ref[...], unroll=UNROLL)

    def bwd(j, b):
        i = steps - 1 - j
        e = jnp.exp(-(gn_ref[i] * r))
        b = e * b + up_ref[pl.ds(i, segs, stride=steps), :]
        adj_ref[0, pl.ds(i, segs, stride=steps), :] = b
        return b

    lax.fori_loop(0, steps, bwd, ib_ref[...], unroll=UNROLL)


def _whole(shape):
    return pl.BlockSpec(shape, lambda j: (0,) * len(shape))


def _lane_specs(total, segs):
    return (
        pl.BlockSpec((1, LANES), lambda j: (0, j)),
        pl.BlockSpec((total, LANES), lambda j: (0, j)),
        pl.BlockSpec((segs, LANES), lambda j: (0, j)),
    )


def local_summaries(g3, gn3, rates2, drive, up):
    total, width = drive.shape
    steps, segs, _ = g3.shape
    r_spec, col, small = _lane_specs(total, segs)
    seg_shape = jax.ShapeDtypeStruct((segs, width), jnp.float32)
    return pl.pallas_call(
        _summary_kernel,
        grid=(width // LANES,),
        in_specs=[_whole(g3.shape), _whole(gn3.shape), r_spec, col, col],
        out_specs=[small] * 4,
        out_shape=[seg_shape] * 4,
    )(g3, gn3, rates2, drive, up)


def sweeps(g3, gn3, rates2, drive, up, init_f, init_b):
    total, width = drive.shape
    steps, segs, _ = g3.shape
    chunks = width // LANES
    r_spec, col, small = _lane_specs(total, segs)
    full = jax.ShapeDtypeStruct((chunks, total, LANES), jnp.float32)
    out = pl.BlockSpec((1, total, LANES), lambda j: (j, 0, 0))
    return pl.pallas_call(
        _sweep_kernel,
        grid=(chunks,),
        in_specs=[_whole(g3.shape), _whole(gn3.shape), r_spec, small, small, col, col],
        out_specs=[out, out],
        out_shape=[full, full],
    )(g3, gn3, rates2, init_f, init_b, drive, up)


def _pick(x, index):
    return lax.dynamic_index_in_dim(x, index, 0, keepdims=False)


def chan_reduce(partial_t):
    ys = lax.axis_size("cy")
    cores = lax.axis_size("cc")
    y = lax.axis_index("cy")
    core = lax.axis_index("cc")
    dmodel, total = partial_t.shape
    blk = dmodel // (ys * cores)
    parts = partial_t.reshape(ys, cores, blk, total).transpose(1, 0, 2, 3)
    mine = _pick(parts, core).astype(jnp.float32)
    other = _pick(parts, (core + 1) % cores)
    swap = [(i, (i + 1) % cores) for i in range(cores)]
    acc = mine + lax.ppermute(other, "cc", swap).astype(jnp.float32)
    half = total // 2
    ahead = acc[:, :, :half]
    behind = acc[:, :, half:]
    up_ring = [(i, (i + 1) % ys) for i in range(ys)]
    down_ring = [(i, (i - 1) % ys) for i in range(ys)]
    buf_a = _pick(ahead, (y - 1) % ys)
    buf_b = _pick(behind, (y + 1) % ys)
    for k in range(ys - 1):
        got_a = lax.ppermute(buf_a.astype(jnp.bfloat16), "cy", up_ring)
        got_b = lax.ppermute(buf_b.astype(jnp.bfloat16), "cy", down_ring)
        buf_a = _pick(ahead, (y - k - 2) % ys) + got_a.astype(jnp.float32)
        buf_b = _pick(behind, (y + k + 2) % ys) + got_b.astype(jnp.float32)
    return jnp.concatenate([buf_a, buf_b], 1).astype(jnp.bfloat16)


def local(inputs, gaps, rates, w_in, w_out, cotangent):
    total = inputs.shape[0]
    width = rates.shape[0]
    segs = SEGMENTS
    steps = total // segs
    peers = lax.axis_size(SEQ)
    place = lax.axis_index(SEQ)
    factor = 1.0 / math.sqrt(total * peers)

    gain = jnp.sqrt(-jnp.expm1(-2.0 * gaps[:, None] * rates[None, :]))
    drive = gain * jnp.dot(inputs, w_in, preferred_element_type=jnp.float32)
    upstream = lax.dot_general(
        cotangent, w_out, (((1,), (1,)), ((), ())), preferred_element_type=jnp.float32
    )
    gaps_next = jnp.concatenate([gaps[1:], jnp.zeros((1,), jnp.float32)], 0)
    g3 = gaps.reshape(segs, steps).T[:, :, None]
    gn3 = gaps_next.reshape(segs, steps).T[:, :, None]
    rates2 = rates[None, :]

    fa, fb, ba, bb = local_summaries(g3, gn3, rates2, drive, up=upstream)

    end_state = jnp.zeros((width,), jnp.float32)
    block_decay = jnp.ones((width,), jnp.float32)
    for s in range(segs):
        end_state = fb[s] + fa[s] * end_state
        block_decay = block_decay * fa[s]
    first_adj = jnp.zeros((width,), jnp.float32)
    for s in reversed(range(segs)):
        first_adj = bb[s] + ba[s] * first_adj
    start_adj = jnp.exp(-gaps[0] * rates) * first_adj

    summary = jnp.stack([block_decay, end_state, start_adj], 0)
    gathered = lax.all_gather(lax.all_gather(summary, "sz"), "sx").reshape(peers, 3, width)
    carry_in = jnp.zeros((width,), jnp.float32)
    for q in range(peers):
        new = gathered[q, 1] + gathered[q, 0] * carry_in
        carry_in = jnp.where(q < place, new, carry_in)
    right_in = jnp.zeros((width,), jnp.float32)
    for q in reversed(range(peers)):
        new = gathered[q, 2] + gathered[q, 0] * right_in
        right_in = jnp.where(q > place, new, right_in)

    inits_f = []
    e = carry_in
    for s in range(segs):
        inits_f.append(e)
        e = fb[s] + fa[s] * e
    inits_b = [None] * segs
    v = right_in
    for s in reversed(range(segs)):
        inits_b[s] = v
        v = bb[s] + ba[s] * v
    init_f = jnp.stack(inits_f, 0)
    init_b = jnp.stack(inits_b, 0)

    state, adjoint = sweeps(g3, gn3, rates2, drive, upstream, init_f, init_b)
    chunks = width // LANES
    gain3 = gain.reshape(total, chunks, LANES).transpose(1, 0, 2)
    drive_grad = (gain3 * adjoint).astype(jnp.bfloat16)
    state_low = state.astype(jnp.bfloat16)
    in_term = lax.dot_general(
        inputs, drive_grad, (((0,), (1,)), ((), ())), preferred_element_type=jnp.float32
    ).reshape(inputs.shape[1], width) * factor
    out_term = lax.dot_general(
        cotangent, state_low, (((0,), (1,)), ((), ())), preferred_element_type=jnp.float32
    ).reshape(cotangent.shape[1], width) * factor
    joined = jnp.concatenate([in_term, out_term], 1).astype(jnp.bfloat16)
    joined = lax.psum_scatter(joined, "sx", scatter_dimension=0, tiled=True)
    joined = lax.psum_scatter(joined, "sz", scatter_dimension=0, tiled=True).astype(jnp.float32)
    d_w_in = joined[:, :width]
    d_w_out = joined[:, width:].T
    w_in3 = w_in.reshape(w_in.shape[0], chunks, LANES)
    partial_t = lax.dot_general(
        w_in3, drive_grad, (((1, 2), (0, 2)), ((), ())), preferred_element_type=jnp.float32
    ).astype(jnp.bfloat16)
    d_inputs = chan_reduce(partial_t).T
    return (d_inputs, d_w_in, d_w_out)


SEQ = ("sx", "sz")
CHAN = ("cy", "cc")


def solution(mesh):
    grid = mesh.devices
    seq_size, chan_size = grid.shape
    z_size = len({d.coords[2] for d in grid[:, 0]})
    core_size = len({d.core_on_chip for d in grid[0, :]})
    split = Mesh(
        grid.reshape(seq_size // z_size, z_size, chan_size // core_size, core_size),
        ("sx", "sz", "cy", "cc"),
    )
    placed = (P(SEQ, None), P(SEQ), P(CHAN), P(None, CHAN), P(CHAN, None), P(SEQ, None))
    return jax.shard_map(
        local,
        mesh=split,
        in_specs=placed,
        out_specs=(P(SEQ, CHAN), P(SEQ, CHAN), P(CHAN, SEQ)),
        check_vma=False,
    )
```

```python
import math

import jax
import jax.numpy as jnp
from jax import lax
from jax.experimental import pallas as pl
from jax.experimental.pallas import tpu as pltpu
from jax.sharding import Mesh, PartitionSpec as P

SEGMENTS = 8
LANES = 128
UNROLL = 8


def _summary_kernel(g_ref, gn_ref, r_ref, *refs):
    chunks = (len(refs) - 4) // 2
    drive_refs = refs[:chunks]
    up_refs = refs[chunks:2 * chunks]
    fa_ref, fb_ref, ba_ref, bb_ref = refs[2 * chunks:]
    steps, segs, _ = g_ref.shape
    rs = [r_ref[:, pl.ds(k * LANES, LANES)] for k in range(chunks)]
    ones = tuple(jnp.ones((segs, LANES), jnp.float32) for _ in range(chunks))
    zeros = tuple(jnp.zeros((segs, LANES), jnp.float32) for _ in range(chunks))

    def fwd(i, carry):
        a, b = carry
        g = g_ref[i]
        new_a, new_b = [], []
        for k in range(chunks):
            d = jnp.exp(-(g * rs[k]))
            x = drive_refs[k][pl.ds(i, segs, stride=steps), :]
            new_a.append(a[k] * d)
            new_b.append(d * b[k] + x)
        return (tuple(new_a), tuple(new_b))

    a, b = lax.fori_loop(0, steps, fwd, (ones, zeros), unroll=UNROLL)
    for k in range(chunks):
        fa_ref[:, pl.ds(k * LANES, LANES)] = a[k]
        fb_ref[:, pl.ds(k * LANES, LANES)] = b[k]

    def bwd(j, carry):
        a, b = carry
        i = steps - 1 - j
        g = gn_ref[i]
        new_a, new_b = [], []
        for k in range(chunks):
            e = jnp.exp(-(g * rs[k]))
            u = up_refs[k][pl.ds(i, segs, stride=steps), :]
            new_a.append(a[k] * e)
            new_b.append(e * b[k] + u)
        return (tuple(new_a), tuple(new_b))

    a, b = lax.fori_loop(0, steps, bwd, (ones, zeros), unroll=UNROLL)
    for k in range(chunks):
        ba_ref[:, pl.ds(k * LANES, LANES)] = a[k]
        bb_ref[:, pl.ds(k * LANES, LANES)] = b[k]


def _sweep_kernel(g_ref, gn_ref, r_ref, if_ref, ib_ref, *refs):
    chunks = (len(refs) - 2) // 2
    drive_refs = refs[:chunks]
    up_refs = refs[chunks:2 * chunks]
    st_ref, adj_ref = refs[2 * chunks:]
    steps, segs, _ = g_ref.shape
    rs = [r_ref[:, pl.ds(k * LANES, LANES)] for k in range(chunks)]

    def fwd(i, b):
        g = g_ref[i]
        out = []
        for k in range(chunks):
            d = jnp.exp(-(g * rs[k]))
            v = d * b[k] + drive_refs[k][pl.ds(i, segs, stride=steps), :]
            st_ref[k, pl.ds(i, segs, stride=steps), :] = v
            out.append(v)
        return tuple(out)

    init = tuple(if_ref[:, pl.ds(k * LANES, LANES)] for k in range(chunks))
    lax.fori_loop(0, steps, fwd, init, unroll=UNROLL)

    def bwd(j, b):
        i = steps - 1 - j
        g = gn_ref[i]
        out = []
        for k in range(chunks):
            e = jnp.exp(-(g * rs[k]))
            v = e * b[k] + up_refs[k][pl.ds(i, segs, stride=steps), :]
            adj_ref[k, pl.ds(i, segs, stride=steps), :] = v
            out.append(v)
        return tuple(out)

    init = tuple(ib_ref[:, pl.ds(k * LANES, LANES)] for k in range(chunks))
    lax.fori_loop(0, steps, bwd, init, unroll=UNROLL)


def _column_specs(total, width):
    return [pl.BlockSpec((total, LANES), lambda j, k=k: (0, k)) for k in range(width // LANES)]


def _whole(shape):
    return pl.BlockSpec(shape, lambda j: (0,) * len(shape))


def local_summaries(g3, gn3, rates2, drive, up):
    total, width = drive.shape
    steps, segs, _ = g3.shape
    chunks = width // LANES
    cols = _column_specs(total, width)
    seg_shape = jax.ShapeDtypeStruct((segs, width), jnp.float32)
    return pl.pallas_call(
        _summary_kernel,
        grid=(1,),
        in_specs=[_whole(g3.shape), _whole(gn3.shape), _whole(rates2.shape)] + cols + cols,
        out_specs=[_whole((segs, width))] * 4,
        out_shape=[seg_shape] * 4,
        compiler_params=pltpu.CompilerParams(vmem_limit_bytes=48 * 1024 * 1024),
    )(g3, gn3, rates2, *([drive] * chunks), *([up] * chunks))


def sweeps(g3, gn3, rates2, drive, up, init_f, init_b):
    total, width = drive.shape
    steps, segs, _ = g3.shape
    chunks = width // LANES
    cols = _column_specs(total, width)
    full = jax.ShapeDtypeStruct((chunks, total, LANES), jnp.float32)
    return pl.pallas_call(
        _sweep_kernel,
        grid=(1,),
        in_specs=[_whole(g3.shape), _whole(gn3.shape), _whole(rates2.shape),
                  _whole(init_f.shape), _whole(init_b.shape)] + cols + cols,
        out_specs=[_whole(full.shape)] * 2,
        out_shape=[full, full],
        compiler_params=pltpu.CompilerParams(vmem_limit_bytes=48 * 1024 * 1024),
    )(g3, gn3, rates2, init_f, init_b, *([drive] * chunks), *([up] * chunks))


def _pick(x, index):
    return lax.dynamic_index_in_dim(x, index, 0, keepdims=False)


def chan_reduce(partial_t):
    ys = lax.axis_size("cy")
    cores = lax.axis_size("cc")
    y = lax.axis_index("cy")
    core = lax.axis_index("cc")
    dmodel, total = partial_t.shape
    blk = dmodel // (ys * cores)
    parts = partial_t.reshape(cores, ys, blk, total)
    mine = _pick(parts, core).astype(jnp.float32)
    other = _pick(parts, (core + 1) % cores)
    swap = [(i, (i + 1) % cores) for i in range(cores)]
    acc = mine + lax.ppermute(other, "cc", swap).astype(jnp.float32)
    half = total // 2
    ahead = acc[:, :, :half]
    behind = acc[:, :, half:]
    up_ring = [(i, (i + 1) % ys) for i in range(ys)]
    down_ring = [(i, (i - 1) % ys) for i in range(ys)]
    buf_a = _pick(ahead, (y - 1) % ys)
    buf_b = _pick(behind, (y + 1) % ys)
    for k in range(ys - 1):
        got_a = lax.ppermute(buf_a.astype(jnp.bfloat16), "cy", up_ring)
        got_b = lax.ppermute(buf_b.astype(jnp.bfloat16), "cy", down_ring)
        buf_a = _pick(ahead, (y - k - 2) % ys) + got_a.astype(jnp.float32)
        buf_b = _pick(behind, (y + k + 2) % ys) + got_b.astype(jnp.float32)
    return jnp.concatenate([buf_a, buf_b], 1).astype(jnp.bfloat16)


def local(inputs, gaps, rates, w_in, w_out, cotangent):
    total = inputs.shape[0]
    width = rates.shape[0]
    segs = SEGMENTS
    steps = total // segs
    peers = lax.axis_size(SEQ)
    place = lax.axis_index(SEQ)
    factor = 1.0 / math.sqrt(total * peers)

    gain = jnp.sqrt(-jnp.expm1(-2.0 * gaps[:, None] * rates[None, :]))
    drive = gain * jnp.dot(inputs, w_in, preferred_element_type=jnp.float32)
    upstream = lax.dot_general(
        cotangent, w_out, (((1,), (1,)), ((), ())), preferred_element_type=jnp.float32
    )
    gaps_next = jnp.concatenate([gaps[1:], jnp.zeros((1,), jnp.float32)], 0)
    g3 = gaps.reshape(segs, steps).T[:, :, None]
    gn3 = gaps_next.reshape(segs, steps).T[:, :, None]
    rates2 = rates[None, :]

    fa, fb, ba, bb = local_summaries(g3, gn3, rates2, drive, up=upstream)

    end_state = jnp.zeros((width,), jnp.float32)
    block_decay = jnp.ones((width,), jnp.float32)
    for s in range(segs):
        end_state = fb[s] + fa[s] * end_state
        block_decay = block_decay * fa[s]
    first_adj = jnp.zeros((width,), jnp.float32)
    for s in reversed(range(segs)):
        first_adj = bb[s] + ba[s] * first_adj
    start_adj = jnp.exp(-gaps[0] * rates) * first_adj

    summary = jnp.stack([block_decay, end_state, start_adj], 0)
    gathered = lax.all_gather(lax.all_gather(summary, "sz"), "sx").reshape(peers, 3, width)
    carry_in = jnp.zeros((width,), jnp.float32)
    for q in range(peers):
        new = gathered[q, 1] + gathered[q, 0] * carry_in
        carry_in = jnp.where(q < place, new, carry_in)
    right_in = jnp.zeros((width,), jnp.float32)
    for q in reversed(range(peers)):
        new = gathered[q, 2] + gathered[q, 0] * right_in
        right_in = jnp.where(q > place, new, right_in)

    inits_f = []
    e = carry_in
    for s in range(segs):
        inits_f.append(e)
        e = fb[s] + fa[s] * e
    inits_b = [None] * segs
    v = right_in
    for s in reversed(range(segs)):
        inits_b[s] = v
        v = bb[s] + ba[s] * v
    init_f = jnp.stack(inits_f, 0)
    init_b = jnp.stack(inits_b, 0)

    state, adjoint = sweeps(g3, gn3, rates2, drive, upstream, init_f, init_b)
    chunks = width // LANES
    gain3 = gain.reshape(total, chunks, LANES).transpose(1, 0, 2)
    drive_grad = (gain3 * adjoint).astype(jnp.bfloat16)
    state_low = state.astype(jnp.bfloat16)
    in_term = lax.dot_general(
        inputs, drive_grad, (((0,), (1,)), ((), ())), preferred_element_type=jnp.float32
    ).reshape(inputs.shape[1], width) * factor
    out_term = lax.dot_general(
        cotangent, state_low, (((0,), (1,)), ((), ())), preferred_element_type=jnp.float32
    ).reshape(cotangent.shape[1], width) * factor
    joined = jnp.concatenate([in_term, out_term], 1).astype(jnp.bfloat16)
    joined = lax.psum_scatter(joined, "sx", scatter_dimension=0, tiled=True)
    joined = lax.psum_scatter(joined, "sz", scatter_dimension=0, tiled=True).astype(jnp.float32)
    d_w_in = joined[:, :width]
    d_w_out = joined[:, width:].T
    ys = lax.axis_size("cy")
    cores = lax.axis_size("cc")
    dmodel = w_in.shape[0]
    w_rows = (
        w_in.reshape(ys, cores, dmodel // (ys * cores), width)
        .transpose(1, 0, 2, 3)
        .reshape(dmodel, chunks, LANES)
    )
    partial_t = lax.dot_general(
        w_rows, drive_grad, (((1, 2), (0, 2)), ((), ())), preferred_element_type=jnp.float32
    ).astype(jnp.bfloat16)
    d_inputs = chan_reduce(partial_t).T
    return (d_inputs, d_w_in, d_w_out)


SEQ = ("sx", "sz")
CHAN = ("cy", "cc")


def solution(mesh):
    grid = mesh.devices
    seq_size, chan_size = grid.shape
    z_size = len({d.coords[2] for d in grid[:, 0]})
    core_size = len({d.core_on_chip for d in grid[0, :]})
    split = Mesh(
        grid.reshape(seq_size // z_size, z_size, chan_size // core_size, core_size),
        ("sx", "sz", "cy", "cc"),
    )
    placed = (P(SEQ, None), P(SEQ), P(CHAN), P(None, CHAN), P(CHAN, None), P(SEQ, None))
    return jax.shard_map(
        local,
        mesh=split,
        in_specs=placed,
        out_specs=(P(SEQ, CHAN), P(SEQ, CHAN), P(CHAN, SEQ)),
        check_vma=False,
    )
```

```python
import math

import jax
import jax.numpy as jnp
from jax import lax
from jax.experimental import pallas as pl
from jax.experimental.pallas import tpu as pltpu
from jax.sharding import Mesh, PartitionSpec as P

SEGMENTS = 8
LANES = 128
UNROLL = 8


def _summary_kernel(g_ref, gn_ref, r_ref, drive_refs, up_refs, fa_ref, fb_ref, ba_ref, bb_ref):
    chunks = drive_refs.shape[0]
    steps, segs, _ = g_ref.shape
    rs = [r_ref[:, pl.ds(k * LANES, LANES)] for k in range(chunks)]
    ones = tuple(jnp.ones((segs, LANES), jnp.float32) for _ in range(chunks))
    zeros = tuple(jnp.zeros((segs, LANES), jnp.float32) for _ in range(chunks))

    def fwd(i, carry):
        a, b = carry
        g = g_ref[i]
        new_a, new_b = [], []
        for k in range(chunks):
            d = jnp.exp(-(g * rs[k]))
            x = drive_refs[k, pl.ds(i, segs, stride=steps), :]
            new_a.append(a[k] * d)
            new_b.append(d * b[k] + x)
        return (tuple(new_a), tuple(new_b))

    a, b = lax.fori_loop(0, steps, fwd, (ones, zeros), unroll=UNROLL)
    for k in range(chunks):
        fa_ref[:, pl.ds(k * LANES, LANES)] = a[k]
        fb_ref[:, pl.ds(k * LANES, LANES)] = b[k]

    def bwd(j, carry):
        a, b = carry
        i = steps - 1 - j
        g = gn_ref[i]
        new_a, new_b = [], []
        for k in range(chunks):
            e = jnp.exp(-(g * rs[k]))
            u = up_refs[k, pl.ds(i, segs, stride=steps), :]
            new_a.append(a[k] * e)
            new_b.append(e * b[k] + u)
        return (tuple(new_a), tuple(new_b))

    a, b = lax.fori_loop(0, steps, bwd, (ones, zeros), unroll=UNROLL)
    for k in range(chunks):
        ba_ref[:, pl.ds(k * LANES, LANES)] = a[k]
        bb_ref[:, pl.ds(k * LANES, LANES)] = b[k]


def _sweep_kernel(g_ref, gn_ref, r_ref, if_ref, ib_ref, drive_refs, up_refs, st_ref, adj_ref):
    chunks = drive_refs.shape[0]
    steps, segs, _ = g_ref.shape
    rs = [r_ref[:, pl.ds(k * LANES, LANES)] for k in range(chunks)]

    def fwd(i, b):
        g = g_ref[i]
        out = []
        for k in range(chunks):
            d = jnp.exp(-(g * rs[k]))
            v = d * b[k] + drive_refs[k, pl.ds(i, segs, stride=steps), :]
            st_ref[k, pl.ds(i, segs, stride=steps), :] = v
            out.append(v)
        return tuple(out)

    init = tuple(if_ref[:, pl.ds(k * LANES, LANES)] for k in range(chunks))
    lax.fori_loop(0, steps, fwd, init, unroll=UNROLL)

    def bwd(j, b):
        i = steps - 1 - j
        g = gn_ref[i]
        out = []
        for k in range(chunks):
            e = jnp.exp(-(g * rs[k]))
            v = e * b[k] + up_refs[k, pl.ds(i, segs, stride=steps), :]
            adj_ref[k, pl.ds(i, segs, stride=steps), :] = v
            out.append(v)
        return tuple(out)

    init = tuple(ib_ref[:, pl.ds(k * LANES, LANES)] for k in range(chunks))
    lax.fori_loop(0, steps, bwd, init, unroll=UNROLL)


def _column_specs(total, width):
    return [pl.BlockSpec((total, LANES), lambda j, k=k: (0, k)) for k in range(width // LANES)]


def _whole(shape):
    return pl.BlockSpec(shape, lambda j: (0,) * len(shape))


def local_summaries(g3, gn3, rates2, drive, up):
    chunks, total, lanes = drive.shape
    width = chunks * lanes
    steps, segs, _ = g3.shape
    cols = [_whole(drive.shape)]
    seg_shape = jax.ShapeDtypeStruct((segs, width), jnp.float32)
    return pl.pallas_call(
        _summary_kernel,
        grid=(1,),
        in_specs=[_whole(g3.shape), _whole(gn3.shape), _whole(rates2.shape)] + cols + cols,
        out_specs=[_whole((segs, width))] * 4,
        out_shape=[seg_shape] * 4,
        compiler_params=pltpu.CompilerParams(vmem_limit_bytes=48 * 1024 * 1024),
    )(g3, gn3, rates2, drive, up)


def sweeps(g3, gn3, rates2, drive, up, init_f, init_b):
    chunks, total, lanes = drive.shape
    steps, segs, _ = g3.shape
    cols = [_whole(drive.shape)]
    full = jax.ShapeDtypeStruct((chunks, total, LANES), jnp.float32)
    return pl.pallas_call(
        _sweep_kernel,
        grid=(1,),
        in_specs=[_whole(g3.shape), _whole(gn3.shape), _whole(rates2.shape),
                  _whole(init_f.shape), _whole(init_b.shape)] + cols + cols,
        out_specs=[_whole(full.shape)] * 2,
        out_shape=[full, full],
        compiler_params=pltpu.CompilerParams(vmem_limit_bytes=48 * 1024 * 1024),
    )(g3, gn3, rates2, init_f, init_b, drive, up)


def _pick(x, index):
    return lax.dynamic_index_in_dim(x, index, 0, keepdims=False)


def chan_reduce(partial_t):
    ys = lax.axis_size("cy")
    cores = lax.axis_size("cc")
    y = lax.axis_index("cy")
    core = lax.axis_index("cc")
    dmodel, total = partial_t.shape
    blk = dmodel // (ys * cores)
    parts = partial_t.reshape(ys, cores, blk, total).transpose(1, 0, 2, 3)
    mine = _pick(parts, core).astype(jnp.float32)
    other = _pick(parts, (core + 1) % cores)
    swap = [(i, (i + 1) % cores) for i in range(cores)]
    acc = mine + lax.ppermute(other, "cc", swap).astype(jnp.float32)
    half = total // 2
    ahead = acc[:, :, :half]
    behind = acc[:, :, half:]
    up_ring = [(i, (i + 1) % ys) for i in range(ys)]
    down_ring = [(i, (i - 1) % ys) for i in range(ys)]
    buf_a = _pick(ahead, (y - 1) % ys)
    buf_b = _pick(behind, (y + 1) % ys)
    for k in range(ys - 1):
        got_a = lax.ppermute(buf_a.astype(jnp.bfloat16), "cy", up_ring)
        got_b = lax.ppermute(buf_b.astype(jnp.bfloat16), "cy", down_ring)
        buf_a = _pick(ahead, (y - k - 2) % ys) + got_a.astype(jnp.float32)
        buf_b = _pick(behind, (y + k + 2) % ys) + got_b.astype(jnp.float32)
    return jnp.concatenate([buf_a, buf_b], 1).astype(jnp.bfloat16)


def local(inputs, gaps, rates, w_in, w_out, cotangent):
    total = inputs.shape[0]
    width = rates.shape[0]
    segs = SEGMENTS
    steps = total // segs
    peers = lax.axis_size(SEQ)
    place = lax.axis_index(SEQ)
    factor = 1.0 / math.sqrt(total * peers)

    gain = jnp.sqrt(-jnp.expm1(-2.0 * gaps[:, None] * rates[None, :]))
    drive = gain * jnp.dot(inputs, w_in, preferred_element_type=jnp.float32)
    upstream = lax.dot_general(
        cotangent, w_out, (((1,), (1,)), ((), ())), preferred_element_type=jnp.float32
    )
    chunks = width // LANES
    drive = drive.reshape(total, chunks, LANES).transpose(1, 0, 2)
    upstream = upstream.reshape(total, chunks, LANES).transpose(1, 0, 2)
    gaps_next = jnp.concatenate([gaps[1:], jnp.zeros((1,), jnp.float32)], 0)
    g3 = gaps.reshape(segs, steps).T[:, :, None]
    gn3 = gaps_next.reshape(segs, steps).T[:, :, None]
    rates2 = rates[None, :]

    fa, fb, ba, bb = local_summaries(g3, gn3, rates2, drive, up=upstream)

    end_state = jnp.zeros((width,), jnp.float32)
    block_decay = jnp.ones((width,), jnp.float32)
    for s in range(segs):
        end_state = fb[s] + fa[s] * end_state
        block_decay = block_decay * fa[s]
    first_adj = jnp.zeros((width,), jnp.float32)
    for s in reversed(range(segs)):
        first_adj = bb[s] + ba[s] * first_adj
    start_adj = jnp.exp(-gaps[0] * rates) * first_adj

    summary = jnp.stack([block_decay, end_state, start_adj], 0)
    gathered = lax.all_gather(lax.all_gather(summary, "sz"), "sx").reshape(peers, 3, width)
    carry_in = jnp.zeros((width,), jnp.float32)
    for q in range(peers):
        new = gathered[q, 1] + gathered[q, 0] * carry_in
        carry_in = jnp.where(q < place, new, carry_in)
    right_in = jnp.zeros((width,), jnp.float32)
    for q in reversed(range(peers)):
        new = gathered[q, 2] + gathered[q, 0] * right_in
        right_in = jnp.where(q > place, new, right_in)

    inits_f = []
    e = carry_in
    for s in range(segs):
        inits_f.append(e)
        e = fb[s] + fa[s] * e
    inits_b = [None] * segs
    v = right_in
    for s in reversed(range(segs)):
        inits_b[s] = v
        v = bb[s] + ba[s] * v
    init_f = jnp.stack(inits_f, 0)
    init_b = jnp.stack(inits_b, 0)

    state, adjoint = sweeps(g3, gn3, rates2, drive, upstream, init_f, init_b)
    chunks = width // LANES
    gain3 = gain.reshape(total, chunks, LANES).transpose(1, 0, 2)
    drive_grad = (gain3 * adjoint).astype(jnp.bfloat16)
    state_low = state.astype(jnp.bfloat16)
    in_term = lax.dot_general(
        inputs, drive_grad, (((0,), (1,)), ((), ())), preferred_element_type=jnp.float32
    ).reshape(inputs.shape[1], width) * factor
    out_term = lax.dot_general(
        cotangent, state_low, (((0,), (1,)), ((), ())), preferred_element_type=jnp.float32
    ).reshape(cotangent.shape[1], width) * factor
    joined = jnp.concatenate([in_term, out_term], 1).astype(jnp.bfloat16)
    joined = lax.psum_scatter(joined, "sx", scatter_dimension=0, tiled=True)
    joined = lax.psum_scatter(joined, "sz", scatter_dimension=0, tiled=True).astype(jnp.float32)
    d_w_in = joined[:, :width]
    d_w_out = joined[:, width:].T
    w_in3 = w_in.reshape(w_in.shape[0], chunks, LANES)
    partial_t = lax.dot_general(
        w_in3, drive_grad, (((1, 2), (0, 2)), ((), ())), preferred_element_type=jnp.float32
    ).astype(jnp.bfloat16)
    d_inputs = chan_reduce(partial_t).T
    return (d_inputs, d_w_in, d_w_out)


SEQ = ("sx", "sz")
CHAN = ("cy", "cc")


def solution(mesh):
    grid = mesh.devices
    seq_size, chan_size = grid.shape
    z_size = len({d.coords[2] for d in grid[:, 0]})
    core_size = len({d.core_on_chip for d in grid[0, :]})
    split = Mesh(
        grid.reshape(seq_size // z_size, z_size, chan_size // core_size, core_size),
        ("sx", "sz", "cy", "cc"),
    )
    placed = (P(SEQ, None), P(SEQ), P(CHAN), P(None, CHAN), P(CHAN, None), P(SEQ, None))
    return jax.shard_map(
        local,
        mesh=split,
        in_specs=placed,
        out_specs=(P(SEQ, CHAN), P(SEQ, CHAN), P(CHAN, SEQ)),
        check_vma=False,
    )
```

```python
import math

import jax
import jax.numpy as jnp
from jax import lax
from jax.experimental import pallas as pl
from jax.experimental.pallas import tpu as pltpu
from jax.sharding import Mesh, PartitionSpec as P

SEGMENTS = 8
LANES = 128
UNROLL = 8


def _summary_kernel(g_ref, gn_ref, r_ref, drive_ref, up_ref, fa_ref, fb_ref, ba_ref, bb_ref):
    steps, segs, _ = g_ref.shape
    r = r_ref[...]
    ones = jnp.ones(fa_ref.shape, jnp.float32)
    zeros = jnp.zeros(fb_ref.shape, jnp.float32)

    def fwd(i, carry):
        a, b = carry
        d = jnp.exp(-(g_ref[i] * r))
        x = drive_ref[pl.ds(pl.multiple_of(i * segs, segs), segs), :]
        return (a * d, d * b + x)

    a, b = lax.fori_loop(0, steps, fwd, (ones, zeros), unroll=UNROLL)
    fa_ref[...] = a
    fb_ref[...] = b

    def bwd(j, carry):
        a, b = carry
        i = steps - 1 - j
        e = jnp.exp(-(gn_ref[i] * r))
        u = up_ref[pl.ds(pl.multiple_of(i * segs, segs), segs), :]
        return (a * e, e * b + u)

    a, b = lax.fori_loop(0, steps, bwd, (ones, zeros), unroll=UNROLL)
    ba_ref[...] = a
    bb_ref[...] = b


def _sweep_kernel(g_ref, gn_ref, r_ref, if_ref, ib_ref, drive_ref, up_ref, st_ref, adj_ref):
    steps, segs, _ = g_ref.shape
    r = r_ref[...]

    def fwd(i, b):
        rows = pl.ds(pl.multiple_of(i * segs, segs), segs)
        d = jnp.exp(-(g_ref[i] * r))
        b = d * b + drive_ref[rows, :]
        st_ref[rows, :] = b
        return b

    lax.fori_loop(0, steps, fwd, if_ref[...], unroll=UNROLL)

    def bwd(j, b):
        i = steps - 1 - j
        rows = pl.ds(pl.multiple_of(i * segs, segs), segs)
        e = jnp.exp(-(gn_ref[i] * r))
        b = e * b + up_ref[rows, :]
        adj_ref[rows, :] = b
        return b

    lax.fori_loop(0, steps, bwd, ib_ref[...], unroll=UNROLL)


def _whole(shape):
    return pl.BlockSpec(shape, lambda j: (0,) * len(shape))


def local_summaries(g3, gn3, rates2, drive, up):
    total, width = drive.shape
    steps, segs, _ = g3.shape
    seg_shape = jax.ShapeDtypeStruct((segs, width), jnp.float32)
    return pl.pallas_call(
        _summary_kernel,
        grid=(1,),
        in_specs=[_whole(g3.shape), _whole(gn3.shape), _whole(rates2.shape),
                  _whole(drive.shape), _whole(up.shape)],
        out_specs=[_whole((segs, width))] * 4,
        out_shape=[seg_shape] * 4,
        compiler_params=pltpu.CompilerParams(vmem_limit_bytes=48 * 1024 * 1024),
    )(g3, gn3, rates2, drive, up)


def sweeps(g3, gn3, rates2, drive, up, init_f, init_b):
    total, width = drive.shape
    full = jax.ShapeDtypeStruct((total, width), jnp.float32)
    return pl.pallas_call(
        _sweep_kernel,
        grid=(1,),
        in_specs=[_whole(g3.shape), _whole(gn3.shape), _whole(rates2.shape),
                  _whole(init_f.shape), _whole(init_b.shape),
                  _whole(drive.shape), _whole(up.shape)],
        out_specs=[_whole(full.shape)] * 2,
        out_shape=[full, full],
        compiler_params=pltpu.CompilerParams(vmem_limit_bytes=48 * 1024 * 1024),
    )(g3, gn3, rates2, init_f, init_b, drive, up)


def _pick(x, index):
    return lax.dynamic_index_in_dim(x, index, 0, keepdims=False)


def chan_reduce(partial_t):
    ys = lax.axis_size("cy")
    cores = lax.axis_size("cc")
    y = lax.axis_index("cy")
    core = lax.axis_index("cc")
    dmodel, total = partial_t.shape
    blk = dmodel // (ys * cores)
    parts = partial_t.reshape(ys, cores, blk, total).transpose(1, 0, 2, 3)
    mine = _pick(parts, core).astype(jnp.float32)
    other = _pick(parts, (core + 1) % cores)
    swap = [(i, (i + 1) % cores) for i in range(cores)]
    acc = mine + lax.ppermute(other, "cc", swap).astype(jnp.float32)
    half = total // 2
    ahead = acc[:, :, :half]
    behind = acc[:, :, half:]
    up_ring = [(i, (i + 1) % ys) for i in range(ys)]
    down_ring = [(i, (i - 1) % ys) for i in range(ys)]
    buf_a = _pick(ahead, (y - 1) % ys)
    buf_b = _pick(behind, (y + 1) % ys)
    for k in range(ys - 1):
        got_a = lax.ppermute(buf_a.astype(jnp.bfloat16), "cy", up_ring)
        got_b = lax.ppermute(buf_b.astype(jnp.bfloat16), "cy", down_ring)
        buf_a = _pick(ahead, (y - k - 2) % ys) + got_a.astype(jnp.float32)
        buf_b = _pick(behind, (y + k + 2) % ys) + got_b.astype(jnp.float32)
    return jnp.concatenate([buf_a, buf_b], 1).astype(jnp.bfloat16)


def local(inputs, gaps, rates, w_in, w_out, cotangent):
    total = inputs.shape[0]
    width = rates.shape[0]
    segs = SEGMENTS
    steps = total // segs
    peers = lax.axis_size(SEQ)
    place = lax.axis_index(SEQ)
    factor = 1.0 / math.sqrt(total * peers)

    def interleave(x):
        return x.reshape((segs, steps) + x.shape[1:]).swapaxes(0, 1).reshape(x.shape)

    x_rows = interleave(inputs)
    c_rows = interleave(cotangent)
    g_rows = interleave(gaps)
    gain = jnp.sqrt(-jnp.expm1(-2.0 * g_rows[:, None] * rates[None, :]))
    drive = gain * jnp.dot(x_rows, w_in, preferred_element_type=jnp.float32)
    upstream = lax.dot_general(
        c_rows, w_out, (((1,), (1,)), ((), ())), preferred_element_type=jnp.float32
    )
    gaps_next = jnp.concatenate([gaps[1:], jnp.zeros((1,), jnp.float32)], 0)
    g3 = g_rows.reshape(steps, segs)[:, :, None]
    gn3 = interleave(gaps_next).reshape(steps, segs)[:, :, None]
    rates2 = rates[None, :]

    fa, fb, ba, bb = local_summaries(g3, gn3, rates2, drive, up=upstream)

    end_state = jnp.zeros((width,), jnp.float32)
    block_decay = jnp.ones((width,), jnp.float32)
    for s in range(segs):
        end_state = fb[s] + fa[s] * end_state
        block_decay = block_decay * fa[s]
    first_adj = jnp.zeros((width,), jnp.float32)
    for s in reversed(range(segs)):
        first_adj = bb[s] + ba[s] * first_adj
    start_adj = jnp.exp(-gaps[0] * rates) * first_adj

    summary = jnp.stack([block_decay, end_state, start_adj], 0)
    gathered = lax.all_gather(lax.all_gather(summary, "sz"), "sx").reshape(peers, 3, width)
    carry_in = jnp.zeros((width,), jnp.float32)
    for q in range(peers):
        new = gathered[q, 1] + gathered[q, 0] * carry_in
        carry_in = jnp.where(q < place, new, carry_in)
    right_in = jnp.zeros((width,), jnp.float32)
    for q in reversed(range(peers)):
        new = gathered[q, 2] + gathered[q, 0] * right_in
        right_in = jnp.where(q > place, new, right_in)

    inits_f = []
    e = carry_in
    for s in range(segs):
        inits_f.append(e)
        e = fb[s] + fa[s] * e
    inits_b = [None] * segs
    v = right_in
    for s in reversed(range(segs)):
        inits_b[s] = v
        v = bb[s] + ba[s] * v
    init_f = jnp.stack(inits_f, 0)
    init_b = jnp.stack(inits_b, 0)

    state, adjoint = sweeps(g3, gn3, rates2, drive, upstream, init_f, init_b)
    drive_grad = (gain * adjoint).astype(jnp.bfloat16)
    state_low = state.astype(jnp.bfloat16)
    in_term = lax.dot_general(
        x_rows, drive_grad, (((0,), (0,)), ((), ())), preferred_element_type=jnp.float32
    ) * factor
    out_term = lax.dot_general(
        c_rows, state_low, (((0,), (0,)), ((), ())), preferred_element_type=jnp.float32
    ) * factor
    joined = jnp.concatenate([in_term, out_term], 1).astype(jnp.bfloat16)
    joined = lax.psum_scatter(joined, "sx", scatter_dimension=0, tiled=True)
    joined = lax.psum_scatter(joined, "sz", scatter_dimension=0, tiled=True).astype(jnp.float32)
    d_w_in = joined[:, :width]
    d_w_out = joined[:, width:].T
    partial_t = lax.dot_general(
        w_in, drive_grad, (((1,), (1,)), ((), ())), preferred_element_type=jnp.float32
    ).astype(jnp.bfloat16)
    d_rows = chan_reduce(partial_t).T
    d_inputs = d_rows.reshape((steps, segs) + d_rows.shape[1:]).swapaxes(0, 1).reshape(d_rows.shape)
    return (d_inputs, d_w_in, d_w_out)


SEQ = ("sx", "sz")
CHAN = ("cy", "cc")


def solution(mesh):
    grid = mesh.devices
    seq_size, chan_size = grid.shape
    z_size = len({d.coords[2] for d in grid[:, 0]})
    core_size = len({d.core_on_chip for d in grid[0, :]})
    split = Mesh(
        grid.reshape(seq_size // z_size, z_size, chan_size // core_size, core_size),
        ("sx", "sz", "cy", "cc"),
    )
    placed = (P(SEQ, None), P(SEQ), P(CHAN), P(None, CHAN), P(CHAN, None), P(SEQ, None))
    return jax.shard_map(
        local,
        mesh=split,
        in_specs=placed,
        out_specs=(P(SEQ, CHAN), P(SEQ, CHAN), P(CHAN, SEQ)),
        check_vma=False,
    )
```

```python
import math

import jax
import jax.numpy as jnp
from jax import lax
from jax.experimental import pallas as pl
from jax.experimental.pallas import tpu as pltpu
from jax.sharding import Mesh, PartitionSpec as P

SEGMENTS = 8
LANES = 128
UNROLL = 8


ROWS = 512


def _summary_kernel(g_ref, gn_ref, r_ref, drive_ref, up_ref, fa_ref, fb_ref, ba_ref, bb_ref,
                    fa_s, fb_s, ba_s, bb_s):
    segs = fa_ref.shape[0]
    per = drive_ref.shape[0] // segs
    j = pl.program_id(0)
    last = pl.num_programs(0) - 1
    r = r_ref[...]

    @pl.when(j == 0)
    def _():
        fa_s[...] = jnp.ones(fa_s.shape, jnp.float32)
        fb_s[...] = jnp.zeros(fb_s.shape, jnp.float32)
        ba_s[...] = jnp.ones(ba_s.shape, jnp.float32)
        bb_s[...] = jnp.zeros(bb_s.shape, jnp.float32)

    def fwd(i, carry):
        a, b = carry
        d = jnp.exp(-(g_ref[j * per + i] * r))
        x = drive_ref[pl.ds(pl.multiple_of(i * segs, segs), segs), :]
        return (a * d, d * b + x)

    a, b = lax.fori_loop(0, per, fwd, (fa_s[...], fb_s[...]), unroll=UNROLL)
    fa_s[...] = a
    fb_s[...] = b

    def bwd(k, carry):
        a, b = carry
        i = per - 1 - k
        e = jnp.exp(-(gn_ref[(last - j) * per + i] * r))
        u = up_ref[pl.ds(pl.multiple_of(i * segs, segs), segs), :]
        return (a * e, e * b + u)

    a, b = lax.fori_loop(0, per, bwd, (ba_s[...], bb_s[...]), unroll=UNROLL)
    ba_s[...] = a
    bb_s[...] = b

    @pl.when(j == last)
    def _():
        fa_ref[...] = fa_s[...]
        fb_ref[...] = fb_s[...]
        ba_ref[...] = ba_s[...]
        bb_ref[...] = bb_s[...]


def _sweep_kernel(g_ref, gn_ref, r_ref, if_ref, ib_ref, drive_ref, up_ref, st_ref, adj_ref,
                  f_s, b_s):
    segs = f_s.shape[0]
    per = drive_ref.shape[0] // segs
    j = pl.program_id(0)
    last = pl.num_programs(0) - 1
    r = r_ref[...]

    @pl.when(j == 0)
    def _():
        f_s[...] = if_ref[...]
        b_s[...] = ib_ref[...]

    def fwd(i, b):
        rows = pl.ds(pl.multiple_of(i * segs, segs), segs)
        d = jnp.exp(-(g_ref[j * per + i] * r))
        b = d * b + drive_ref[rows, :]
        st_ref[rows, :] = b
        return b

    f_s[...] = lax.fori_loop(0, per, fwd, f_s[...], unroll=UNROLL)

    def bwd(k, b):
        i = per - 1 - k
        rows = pl.ds(pl.multiple_of(i * segs, segs), segs)
        e = jnp.exp(-(gn_ref[(last - j) * per + i] * r))
        b = e * b + up_ref[rows, :]
        adj_ref[rows, :] = b
        return b

    b_s[...] = lax.fori_loop(0, per, bwd, b_s[...], unroll=UNROLL)


def _whole(shape):
    return pl.BlockSpec(shape, lambda j: (0,) * len(shape))


def _row_specs(total, width):
    blocks = total // ROWS
    ahead = pl.BlockSpec((ROWS, width), lambda j: (j, 0))
    behind = pl.BlockSpec((ROWS, width), lambda j: (blocks - 1 - j, 0))
    return blocks, ahead, behind


def local_summaries(g3, gn3, rates2, drive, up):
    total, width = drive.shape
    steps, segs, _ = g3.shape
    blocks, ahead, behind = _row_specs(total, width)
    seg_shape = jax.ShapeDtypeStruct((segs, width), jnp.float32)
    return pl.pallas_call(
        _summary_kernel,
        grid=(blocks,),
        in_specs=[_whole(g3.shape), _whole(gn3.shape), _whole(rates2.shape), ahead, behind],
        out_specs=[_whole((segs, width))] * 4,
        out_shape=[seg_shape] * 4,
        scratch_shapes=[pltpu.VMEM((segs, width), jnp.float32)] * 4,
    )(g3, gn3, rates2, drive, up)


def sweeps(g3, gn3, rates2, drive, up, init_f, init_b):
    total, width = drive.shape
    steps, segs, _ = g3.shape
    blocks, ahead, behind = _row_specs(total, width)
    full = jax.ShapeDtypeStruct((total, width), jnp.float32)
    return pl.pallas_call(
        _sweep_kernel,
        grid=(blocks,),
        in_specs=[_whole(g3.shape), _whole(gn3.shape), _whole(rates2.shape),
                  _whole(init_f.shape), _whole(init_b.shape), ahead, behind],
        out_specs=[ahead, behind],
        out_shape=[full, full],
        scratch_shapes=[pltpu.VMEM((segs, width), jnp.float32)] * 2,
    )(g3, gn3, rates2, init_f, init_b, drive, up)


def _pick(x, index):
    return lax.dynamic_index_in_dim(x, index, 0, keepdims=False)


def chan_reduce(partial_t):
    ys = lax.axis_size("cy")
    cores = lax.axis_size("cc")
    y = lax.axis_index("cy")
    core = lax.axis_index("cc")
    dmodel, total = partial_t.shape
    blk = dmodel // (ys * cores)
    parts = partial_t.reshape(ys, cores, blk, total).transpose(1, 0, 2, 3)
    mine = _pick(parts, core).astype(jnp.float32)
    other = _pick(parts, (core + 1) % cores)
    swap = [(i, (i + 1) % cores) for i in range(cores)]
    acc = mine + lax.ppermute(other, "cc", swap).astype(jnp.float32)
    half = total // 2
    ahead = acc[:, :, :half]
    behind = acc[:, :, half:]
    up_ring = [(i, (i + 1) % ys) for i in range(ys)]
    down_ring = [(i, (i - 1) % ys) for i in range(ys)]
    buf_a = _pick(ahead, (y - 1) % ys)
    buf_b = _pick(behind, (y + 1) % ys)
    for k in range(ys - 1):
        got_a = lax.ppermute(buf_a.astype(jnp.bfloat16), "cy", up_ring)
        got_b = lax.ppermute(buf_b.astype(jnp.bfloat16), "cy", down_ring)
        buf_a = _pick(ahead, (y - k - 2) % ys) + got_a.astype(jnp.float32)
        buf_b = _pick(behind, (y + k + 2) % ys) + got_b.astype(jnp.float32)
    return jnp.concatenate([buf_a, buf_b], 1).astype(jnp.bfloat16)


def local(inputs, gaps, rates, w_in, w_out, cotangent):
    total = inputs.shape[0]
    width = rates.shape[0]
    segs = SEGMENTS
    steps = total // segs
    peers = lax.axis_size(SEQ)
    place = lax.axis_index(SEQ)
    factor = 1.0 / math.sqrt(total * peers)

    def interleave(x):
        return x.reshape((segs, steps) + x.shape[1:]).swapaxes(0, 1).reshape(x.shape)

    x_rows = interleave(inputs)
    c_rows = interleave(cotangent)
    g_rows = interleave(gaps)
    gain = jnp.sqrt(-jnp.expm1(-2.0 * g_rows[:, None] * rates[None, :]))
    drive = gain * jnp.dot(x_rows, w_in, preferred_element_type=jnp.float32)
    upstream = lax.dot_general(
        c_rows, w_out, (((1,), (1,)), ((), ())), preferred_element_type=jnp.float32
    )
    gaps_next = jnp.concatenate([gaps[1:], jnp.zeros((1,), jnp.float32)], 0)
    g3 = g_rows.reshape(steps, segs)[:, :, None]
    gn3 = interleave(gaps_next).reshape(steps, segs)[:, :, None]
    rates2 = rates[None, :]

    fa, fb, ba, bb = local_summaries(g3, gn3, rates2, drive, up=upstream)

    end_state = jnp.zeros((width,), jnp.float32)
    block_decay = jnp.ones((width,), jnp.float32)
    for s in range(segs):
        end_state = fb[s] + fa[s] * end_state
        block_decay = block_decay * fa[s]
    first_adj = jnp.zeros((width,), jnp.float32)
    for s in reversed(range(segs)):
        first_adj = bb[s] + ba[s] * first_adj
    start_adj = jnp.exp(-gaps[0] * rates) * first_adj

    summary = jnp.stack([block_decay, end_state, start_adj], 0)
    gathered = lax.all_gather(lax.all_gather(summary, "sz"), "sx").reshape(peers, 3, width)
    carry_in = jnp.zeros((width,), jnp.float32)
    for q in range(peers):
        new = gathered[q, 1] + gathered[q, 0] * carry_in
        carry_in = jnp.where(q < place, new, carry_in)
    right_in = jnp.zeros((width,), jnp.float32)
    for q in reversed(range(peers)):
        new = gathered[q, 2] + gathered[q, 0] * right_in
        right_in = jnp.where(q > place, new, right_in)

    inits_f = []
    e = carry_in
    for s in range(segs):
        inits_f.append(e)
        e = fb[s] + fa[s] * e
    inits_b = [None] * segs
    v = right_in
    for s in reversed(range(segs)):
        inits_b[s] = v
        v = bb[s] + ba[s] * v
    init_f = jnp.stack(inits_f, 0)
    init_b = jnp.stack(inits_b, 0)

    state, adjoint = sweeps(g3, gn3, rates2, drive, upstream, init_f, init_b)
    drive_grad = (gain * adjoint).astype(jnp.bfloat16)
    state_low = state.astype(jnp.bfloat16)
    in_term = lax.dot_general(
        x_rows, drive_grad, (((0,), (0,)), ((), ())), preferred_element_type=jnp.float32
    ) * factor
    out_term = lax.dot_general(
        c_rows, state_low, (((0,), (0,)), ((), ())), preferred_element_type=jnp.float32
    ) * factor
    joined = jnp.concatenate([in_term, out_term], 1).astype(jnp.bfloat16)
    joined = lax.psum_scatter(joined, "sx", scatter_dimension=0, tiled=True)
    joined = lax.psum_scatter(joined, "sz", scatter_dimension=0, tiled=True).astype(jnp.float32)
    d_w_in = joined[:, :width]
    d_w_out = joined[:, width:].T
    partial_t = lax.dot_general(
        w_in, drive_grad, (((1,), (1,)), ((), ())), preferred_element_type=jnp.float32
    ).astype(jnp.bfloat16)
    d_rows = chan_reduce(partial_t).T
    d_inputs = d_rows.reshape((steps, segs) + d_rows.shape[1:]).swapaxes(0, 1).reshape(d_rows.shape)
    return (d_inputs, d_w_in, d_w_out)


SEQ = ("sx", "sz")
CHAN = ("cy", "cc")


def solution(mesh):
    grid = mesh.devices
    seq_size, chan_size = grid.shape
    z_size = len({d.coords[2] for d in grid[:, 0]})
    core_size = len({d.core_on_chip for d in grid[0, :]})
    split = Mesh(
        grid.reshape(seq_size // z_size, z_size, chan_size // core_size, core_size),
        ("sx", "sz", "cy", "cc"),
    )
    placed = (P(SEQ, None), P(SEQ), P(CHAN), P(None, CHAN), P(CHAN, None), P(SEQ, None))
    return jax.shard_map(
        local,
        mesh=split,
        in_specs=placed,
        out_specs=(P(SEQ, CHAN), P(SEQ, CHAN), P(CHAN, SEQ)),
        check_vma=False,
    )
```

```python
import math

import jax
import jax.numpy as jnp
from jax import lax
from jax.experimental import pallas as pl
from jax.experimental.pallas import tpu as pltpu
from jax.sharding import Mesh, PartitionSpec as P

SEGMENTS = 8
LANES = 128
UNROLL = 8


def _summary_kernel(g_ref, gn_ref, r_ref, drive_ref, up_ref, fa_ref, fb_ref, ba_ref, bb_ref,
                    dec_ref):
    steps, segs, _ = g_ref.shape
    r = r_ref[...]
    ones = jnp.ones(fa_ref.shape, jnp.float32)
    zeros = jnp.zeros(fb_ref.shape, jnp.float32)

    def fwd(i, carry):
        a, b = carry
        rows = pl.ds(pl.multiple_of(i * segs, segs), segs)
        d = jnp.exp(-(g_ref[i] * r))
        dec_ref[rows, :] = d
        x = drive_ref[rows, :]
        return (a * d, d * b + x)

    a, b = lax.fori_loop(0, steps, fwd, (ones, zeros), unroll=UNROLL)
    fa_ref[...] = a
    fb_ref[...] = b

    dec_ref[pl.ds(steps * segs, segs), :] = jnp.exp(-(gn_ref[steps - 1] * r))

    def bwd(j, carry):
        a, b = carry
        i = steps - 1 - j
        e = dec_ref[pl.ds(pl.multiple_of((i + 1) * segs, segs), segs), :]
        u = up_ref[pl.ds(pl.multiple_of(i * segs, segs), segs), :]
        return (a * e, e * b + u)

    a, b = lax.fori_loop(0, steps, bwd, (ones, zeros), unroll=UNROLL)
    ba_ref[...] = a
    bb_ref[...] = b


def _sweep_kernel(g_ref, gn_ref, r_ref, if_ref, ib_ref, drive_ref, up_ref, st_ref, adj_ref,
                  dec_ref):
    steps, segs, _ = g_ref.shape
    r = r_ref[...]

    def fwd(i, b):
        rows = pl.ds(pl.multiple_of(i * segs, segs), segs)
        d = jnp.exp(-(g_ref[i] * r))
        dec_ref[rows, :] = d
        b = d * b + drive_ref[rows, :]
        st_ref[rows, :] = b
        return b

    lax.fori_loop(0, steps, fwd, if_ref[...], unroll=UNROLL)

    dec_ref[pl.ds(steps * segs, segs), :] = jnp.exp(-(gn_ref[steps - 1] * r))

    def bwd(j, b):
        i = steps - 1 - j
        rows = pl.ds(pl.multiple_of(i * segs, segs), segs)
        e = dec_ref[pl.ds(pl.multiple_of((i + 1) * segs, segs), segs), :]
        b = e * b + up_ref[rows, :]
        adj_ref[rows, :] = b
        return b

    lax.fori_loop(0, steps, bwd, ib_ref[...], unroll=UNROLL)


def _whole(shape):
    return pl.BlockSpec(shape, lambda j: (0,) * len(shape))


def local_summaries(g3, gn3, rates2, drive, up):
    total, width = drive.shape
    steps, segs, _ = g3.shape
    seg_shape = jax.ShapeDtypeStruct((segs, width), jnp.float32)
    return pl.pallas_call(
        _summary_kernel,
        grid=(1,),
        in_specs=[_whole(g3.shape), _whole(gn3.shape), _whole(rates2.shape),
                  _whole(drive.shape), _whole(up.shape)],
        out_specs=[_whole((segs, width))] * 4,
        out_shape=[seg_shape] * 4,
        scratch_shapes=[pltpu.VMEM((total + segs, width), jnp.float32)],
        compiler_params=pltpu.CompilerParams(vmem_limit_bytes=48 * 1024 * 1024),
    )(g3, gn3, rates2, drive, up)


def sweeps(g3, gn3, rates2, drive, up, init_f, init_b):
    total, width = drive.shape
    segs = g3.shape[1]
    full = jax.ShapeDtypeStruct((total, width), jnp.float32)
    return pl.pallas_call(
        _sweep_kernel,
        grid=(1,),
        in_specs=[_whole(g3.shape), _whole(gn3.shape), _whole(rates2.shape),
                  _whole(init_f.shape), _whole(init_b.shape),
                  _whole(drive.shape), _whole(up.shape)],
        out_specs=[_whole(full.shape)] * 2,
        out_shape=[full, full],
        scratch_shapes=[pltpu.VMEM((total + segs, width), jnp.float32)],
        compiler_params=pltpu.CompilerParams(vmem_limit_bytes=48 * 1024 * 1024),
    )(g3, gn3, rates2, init_f, init_b, drive, up)


def _pick(x, index):
    return lax.dynamic_index_in_dim(x, index, 0, keepdims=False)


def chan_reduce(partial_t):
    ys = lax.axis_size("cy")
    cores = lax.axis_size("cc")
    y = lax.axis_index("cy")
    core = lax.axis_index("cc")
    dmodel, total = partial_t.shape
    blk = dmodel // (ys * cores)
    parts = partial_t.reshape(ys, cores, blk, total).transpose(1, 0, 2, 3)
    mine = _pick(parts, core).astype(jnp.float32)
    other = _pick(parts, (core + 1) % cores)
    swap = [(i, (i + 1) % cores) for i in range(cores)]
    acc = mine + lax.ppermute(other, "cc", swap).astype(jnp.float32)
    half = total // 2
    ahead = acc[:, :, :half]
    behind = acc[:, :, half:]
    up_ring = [(i, (i + 1) % ys) for i in range(ys)]
    down_ring = [(i, (i - 1) % ys) for i in range(ys)]
    buf_a = _pick(ahead, (y - 1) % ys)
    buf_b = _pick(behind, (y + 1) % ys)
    for k in range(ys - 1):
        got_a = lax.ppermute(buf_a.astype(jnp.bfloat16), "cy", up_ring)
        got_b = lax.ppermute(buf_b.astype(jnp.bfloat16), "cy", down_ring)
        buf_a = _pick(ahead, (y - k - 2) % ys) + got_a.astype(jnp.float32)
        buf_b = _pick(behind, (y + k + 2) % ys) + got_b.astype(jnp.float32)
    return jnp.concatenate([buf_a, buf_b], 1).astype(jnp.bfloat16)


def local(inputs, gaps, rates, w_in, w_out, cotangent):
    total = inputs.shape[0]
    width = rates.shape[0]
    segs = SEGMENTS
    steps = total // segs
    peers = lax.axis_size(SEQ)
    place = lax.axis_index(SEQ)
    factor = 1.0 / math.sqrt(total * peers)

    def interleave(x):
        return x.reshape((segs, steps) + x.shape[1:]).swapaxes(0, 1).reshape(x.shape)

    x_rows = interleave(inputs)
    c_rows = interleave(cotangent)
    g_rows = interleave(gaps)
    gain = jnp.sqrt(-jnp.expm1(-2.0 * g_rows[:, None] * rates[None, :]))
    drive = gain * jnp.dot(x_rows, w_in, preferred_element_type=jnp.float32)
    upstream = lax.dot_general(
        c_rows, w_out, (((1,), (1,)), ((), ())), preferred_element_type=jnp.float32
    )
    gaps_next = jnp.concatenate([gaps[1:], jnp.zeros((1,), jnp.float32)], 0)
    g3 = g_rows.reshape(steps, segs)[:, :, None]
    gn3 = interleave(gaps_next).reshape(steps, segs)[:, :, None]
    rates2 = rates[None, :]

    fa, fb, ba, bb = local_summaries(g3, gn3, rates2, drive, up=upstream)

    end_state = jnp.zeros((width,), jnp.float32)
    block_decay = jnp.ones((width,), jnp.float32)
    for s in range(segs):
        end_state = fb[s] + fa[s] * end_state
        block_decay = block_decay * fa[s]
    first_adj = jnp.zeros((width,), jnp.float32)
    for s in reversed(range(segs)):
        first_adj = bb[s] + ba[s] * first_adj
    start_adj = jnp.exp(-gaps[0] * rates) * first_adj

    summary = jnp.stack([block_decay, end_state, start_adj], 0)
    gathered = lax.all_gather(lax.all_gather(summary, "sz"), "sx").reshape(peers, 3, width)
    carry_in = jnp.zeros((width,), jnp.float32)
    for q in range(peers):
        new = gathered[q, 1] + gathered[q, 0] * carry_in
        carry_in = jnp.where(q < place, new, carry_in)
    right_in = jnp.zeros((width,), jnp.float32)
    for q in reversed(range(peers)):
        new = gathered[q, 2] + gathered[q, 0] * right_in
        right_in = jnp.where(q > place, new, right_in)

    inits_f = []
    e = carry_in
    for s in range(segs):
        inits_f.append(e)
        e = fb[s] + fa[s] * e
    inits_b = [None] * segs
    v = right_in
    for s in reversed(range(segs)):
        inits_b[s] = v
        v = bb[s] + ba[s] * v
    init_f = jnp.stack(inits_f, 0)
    init_b = jnp.stack(inits_b, 0)

    state, adjoint = sweeps(g3, gn3, rates2, drive, upstream, init_f, init_b)
    drive_grad = (gain * adjoint).astype(jnp.bfloat16)
    state_low = state.astype(jnp.bfloat16)
    in_term = lax.dot_general(
        x_rows, drive_grad, (((0,), (0,)), ((), ())), preferred_element_type=jnp.float32
    ) * factor
    out_term = lax.dot_general(
        c_rows, state_low, (((0,), (0,)), ((), ())), preferred_element_type=jnp.float32
    ) * factor
    joined = jnp.concatenate([in_term, out_term], 1).astype(jnp.bfloat16)
    joined = lax.psum_scatter(joined, "sx", scatter_dimension=0, tiled=True)
    joined = lax.psum_scatter(joined, "sz", scatter_dimension=0, tiled=True).astype(jnp.float32)
    d_w_in = joined[:, :width]
    d_w_out = joined[:, width:].T
    partial_t = lax.dot_general(
        w_in, drive_grad, (((1,), (1,)), ((), ())), preferred_element_type=jnp.float32
    ).astype(jnp.bfloat16)
    d_rows = chan_reduce(partial_t).T
    d_inputs = d_rows.reshape((steps, segs) + d_rows.shape[1:]).swapaxes(0, 1).reshape(d_rows.shape)
    return (d_inputs, d_w_in, d_w_out)


SEQ = ("sx", "sz")
CHAN = ("cy", "cc")


def solution(mesh):
    grid = mesh.devices
    seq_size, chan_size = grid.shape
    z_size = len({d.coords[2] for d in grid[:, 0]})
    core_size = len({d.core_on_chip for d in grid[0, :]})
    split = Mesh(
        grid.reshape(seq_size // z_size, z_size, chan_size // core_size, core_size),
        ("sx", "sz", "cy", "cc"),
    )
    placed = (P(SEQ, None), P(SEQ), P(CHAN), P(None, CHAN), P(CHAN, None), P(SEQ, None))
    return jax.shard_map(
        local,
        mesh=split,
        in_specs=placed,
        out_specs=(P(SEQ, CHAN), P(SEQ, CHAN), P(CHAN, SEQ)),
        check_vma=False,
    )
```

```python
import math

import jax
import jax.numpy as jnp
from jax import lax
from jax.experimental import pallas as pl
from jax.experimental.pallas import tpu as pltpu
from jax.sharding import Mesh, PartitionSpec as P

SEGMENTS = 8
LANES = 128
UNROLL = 8


def _summary_kernel(g_ref, gn_ref, r_ref, drive_ref, up_ref, fb_ref, bb_ref, dec_ref):
    steps, segs, _ = g_ref.shape
    r = r_ref[...]
    zeros = jnp.zeros(fb_ref.shape, jnp.float32)

    def fwd(i, b):
        rows = pl.ds(pl.multiple_of(i * segs, segs), segs)
        d = jnp.exp(-(g_ref[i] * r))
        dec_ref[rows, :] = d
        return d * b + drive_ref[rows, :]

    fb_ref[...] = lax.fori_loop(0, steps, fwd, zeros, unroll=UNROLL)
    dec_ref[pl.ds(steps * segs, segs), :] = jnp.exp(-(gn_ref[steps - 1] * r))

    def bwd(j, b):
        i = steps - 1 - j
        e = dec_ref[pl.ds(pl.multiple_of((i + 1) * segs, segs), segs), :]
        return e * b + up_ref[pl.ds(pl.multiple_of(i * segs, segs), segs), :]

    bb_ref[...] = lax.fori_loop(0, steps, bwd, zeros, unroll=UNROLL)


def _sweep_kernel(g_ref, gn_ref, r_ref, if_ref, ib_ref, drive_ref, up_ref, st_ref, adj_ref,
                  dec_ref):
    steps, segs, _ = g_ref.shape
    r = r_ref[...]

    def fwd(i, b):
        rows = pl.ds(pl.multiple_of(i * segs, segs), segs)
        d = jnp.exp(-(g_ref[i] * r))
        dec_ref[rows, :] = d
        b = d * b + drive_ref[rows, :]
        st_ref[rows, :] = b
        return b

    lax.fori_loop(0, steps, fwd, if_ref[...], unroll=UNROLL)

    dec_ref[pl.ds(steps * segs, segs), :] = jnp.exp(-(gn_ref[steps - 1] * r))

    def bwd(j, b):
        i = steps - 1 - j
        rows = pl.ds(pl.multiple_of(i * segs, segs), segs)
        e = dec_ref[pl.ds(pl.multiple_of((i + 1) * segs, segs), segs), :]
        b = e * b + up_ref[rows, :]
        adj_ref[rows, :] = b
        return b

    lax.fori_loop(0, steps, bwd, ib_ref[...], unroll=UNROLL)


def _whole(shape):
    return pl.BlockSpec(shape, lambda j: (0,) * len(shape))


def local_summaries(g3, gn3, rates2, drive, up):
    total, width = drive.shape
    steps, segs, _ = g3.shape
    seg_shape = jax.ShapeDtypeStruct((segs, width), jnp.float32)
    return pl.pallas_call(
        _summary_kernel,
        grid=(1,),
        in_specs=[_whole(g3.shape), _whole(gn3.shape), _whole(rates2.shape),
                  _whole(drive.shape), _whole(up.shape)],
        out_specs=[_whole((segs, width))] * 2,
        out_shape=[seg_shape] * 2,
        scratch_shapes=[pltpu.VMEM((total + segs, width), jnp.float32)],
        compiler_params=pltpu.CompilerParams(vmem_limit_bytes=48 * 1024 * 1024),
    )(g3, gn3, rates2, drive, up)


def sweeps(g3, gn3, rates2, drive, up, init_f, init_b):
    total, width = drive.shape
    segs = g3.shape[1]
    full = jax.ShapeDtypeStruct((total, width), jnp.float32)
    return pl.pallas_call(
        _sweep_kernel,
        grid=(1,),
        in_specs=[_whole(g3.shape), _whole(gn3.shape), _whole(rates2.shape),
                  _whole(init_f.shape), _whole(init_b.shape),
                  _whole(drive.shape), _whole(up.shape)],
        out_specs=[_whole(full.shape)] * 2,
        out_shape=[full, full],
        scratch_shapes=[pltpu.VMEM((total + segs, width), jnp.float32)],
        compiler_params=pltpu.CompilerParams(vmem_limit_bytes=48 * 1024 * 1024),
    )(g3, gn3, rates2, init_f, init_b, drive, up)


def _pick(x, index):
    return lax.dynamic_index_in_dim(x, index, 0, keepdims=False)


def chan_reduce(partial_t):
    ys = lax.axis_size("cy")
    cores = lax.axis_size("cc")
    y = lax.axis_index("cy")
    core = lax.axis_index("cc")
    dmodel, total = partial_t.shape
    blk = dmodel // (ys * cores)
    parts = partial_t.reshape(ys, cores, blk, total).transpose(1, 0, 2, 3)
    mine = _pick(parts, core).astype(jnp.float32)
    other = _pick(parts, (core + 1) % cores)
    swap = [(i, (i + 1) % cores) for i in range(cores)]
    acc = mine + lax.ppermute(other, "cc", swap).astype(jnp.float32)
    half = total // 2
    ahead = acc[:, :, :half]
    behind = acc[:, :, half:]
    up_ring = [(i, (i + 1) % ys) for i in range(ys)]
    down_ring = [(i, (i - 1) % ys) for i in range(ys)]
    buf_a = _pick(ahead, (y - 1) % ys)
    buf_b = _pick(behind, (y + 1) % ys)
    for k in range(ys - 1):
        got_a = lax.ppermute(buf_a.astype(jnp.bfloat16), "cy", up_ring)
        got_b = lax.ppermute(buf_b.astype(jnp.bfloat16), "cy", down_ring)
        buf_a = _pick(ahead, (y - k - 2) % ys) + got_a.astype(jnp.float32)
        buf_b = _pick(behind, (y + k + 2) % ys) + got_b.astype(jnp.float32)
    return jnp.concatenate([buf_a, buf_b], 1).astype(jnp.bfloat16)


def local(inputs, gaps, rates, w_in, w_out, cotangent):
    total = inputs.shape[0]
    width = rates.shape[0]
    segs = SEGMENTS
    steps = total // segs
    peers = lax.axis_size(SEQ)
    place = lax.axis_index(SEQ)
    factor = 1.0 / math.sqrt(total * peers)

    def interleave(x):
        return x.reshape((segs, steps) + x.shape[1:]).swapaxes(0, 1).reshape(x.shape)

    x_rows = interleave(inputs)
    c_rows = interleave(cotangent)
    g_rows = interleave(gaps)
    gain = jnp.sqrt(-jnp.expm1(-2.0 * g_rows[:, None] * rates[None, :]))
    drive = gain * jnp.dot(x_rows, w_in, preferred_element_type=jnp.float32)
    upstream = lax.dot_general(
        c_rows, w_out, (((1,), (1,)), ((), ())), preferred_element_type=jnp.float32
    )
    gaps_next = jnp.concatenate([gaps[1:], jnp.zeros((1,), jnp.float32)], 0)
    g3 = g_rows.reshape(steps, segs)[:, :, None]
    gn3 = interleave(gaps_next).reshape(steps, segs)[:, :, None]
    rates2 = rates[None, :]

    fb, bb = local_summaries(g3, gn3, rates2, drive, up=upstream)
    fa = jnp.exp(-(g3[:, :, 0].sum(0)[:, None] * rates2))
    ba = jnp.exp(-(gn3[:, :, 0].sum(0)[:, None] * rates2))

    end_state = jnp.zeros((width,), jnp.float32)
    block_decay = jnp.ones((width,), jnp.float32)
    for s in range(segs):
        end_state = fb[s] + fa[s] * end_state
        block_decay = block_decay * fa[s]
    first_adj = jnp.zeros((width,), jnp.float32)
    for s in reversed(range(segs)):
        first_adj = bb[s] + ba[s] * first_adj
    start_adj = jnp.exp(-gaps[0] * rates) * first_adj

    summary = jnp.stack([block_decay, end_state, start_adj], 0)
    gathered = lax.all_gather(lax.all_gather(summary, "sz"), "sx").reshape(peers, 3, width)
    carry_in = jnp.zeros((width,), jnp.float32)
    for q in range(peers):
        new = gathered[q, 1] + gathered[q, 0] * carry_in
        carry_in = jnp.where(q < place, new, carry_in)
    right_in = jnp.zeros((width,), jnp.float32)
    for q in reversed(range(peers)):
        new = gathered[q, 2] + gathered[q, 0] * right_in
        right_in = jnp.where(q > place, new, right_in)

    inits_f = []
    e = carry_in
    for s in range(segs):
        inits_f.append(e)
        e = fb[s] + fa[s] * e
    inits_b = [None] * segs
    v = right_in
    for s in reversed(range(segs)):
        inits_b[s] = v
        v = bb[s] + ba[s] * v
    init_f = jnp.stack(inits_f, 0)
    init_b = jnp.stack(inits_b, 0)

    state, adjoint = sweeps(g3, gn3, rates2, drive, upstream, init_f, init_b)
    drive_grad = (gain * adjoint).astype(jnp.bfloat16)
    state_low = state.astype(jnp.bfloat16)
    in_term = lax.dot_general(
        x_rows, drive_grad, (((0,), (0,)), ((), ())), preferred_element_type=jnp.float32
    ) * factor
    out_term = lax.dot_general(
        c_rows, state_low, (((0,), (0,)), ((), ())), preferred_element_type=jnp.float32
    ) * factor
    joined = jnp.concatenate([in_term, out_term], 1).astype(jnp.bfloat16)
    joined = lax.psum_scatter(joined, "sx", scatter_dimension=0, tiled=True)
    joined = lax.psum_scatter(joined, "sz", scatter_dimension=0, tiled=True).astype(jnp.float32)
    d_w_in = joined[:, :width]
    d_w_out = joined[:, width:].T
    partial_t = lax.dot_general(
        w_in, drive_grad, (((1,), (1,)), ((), ())), preferred_element_type=jnp.float32
    ).astype(jnp.bfloat16)
    d_rows = chan_reduce(partial_t).T
    d_inputs = d_rows.reshape((steps, segs) + d_rows.shape[1:]).swapaxes(0, 1).reshape(d_rows.shape)
    return (d_inputs, d_w_in, d_w_out)


SEQ = ("sx", "sz")
CHAN = ("cy", "cc")


def solution(mesh):
    grid = mesh.devices
    seq_size, chan_size = grid.shape
    z_size = len({d.coords[2] for d in grid[:, 0]})
    core_size = len({d.core_on_chip for d in grid[0, :]})
    split = Mesh(
        grid.reshape(seq_size // z_size, z_size, chan_size // core_size, core_size),
        ("sx", "sz", "cy", "cc"),
    )
    placed = (P(SEQ, None), P(SEQ), P(CHAN), P(None, CHAN), P(CHAN, None), P(SEQ, None))
    return jax.shard_map(
        local,
        mesh=split,
        in_specs=placed,
        out_specs=(P(SEQ, CHAN), P(SEQ, CHAN), P(CHAN, SEQ)),
        check_vma=False,
    )
```

```python
import math

import jax
import jax.numpy as jnp
from jax import lax
from jax.experimental import pallas as pl
from jax.experimental.pallas import tpu as pltpu
from jax.sharding import Mesh, PartitionSpec as P

SEGMENTS = 8
LANES = 128
UNROLL = 8


def _summary_kernel(g_ref, gn_ref, r_ref, drive_ref, up_ref, fa_ref, fb_ref, ba_ref, bb_ref,
                    dec_ref):
    steps, segs, _ = g_ref.shape
    r = r_ref[...]
    ones = jnp.ones(fa_ref.shape, jnp.float32)
    zeros = jnp.zeros(fb_ref.shape, jnp.float32)

    def fwd(i, carry):
        a, b = carry
        rows = pl.ds(pl.multiple_of(i * segs, segs), segs)
        d = jnp.exp(-(g_ref[i] * r))
        dec_ref[rows, :] = d
        x = drive_ref[rows, :]
        return (a * d, d * b + x)

    a, b = lax.fori_loop(0, steps, fwd, (ones, zeros), unroll=UNROLL)
    fa_ref[...] = a
    fb_ref[...] = b

    dec_ref[pl.ds(steps * segs, segs), :] = jnp.exp(-(gn_ref[steps - 1] * r))

    def bwd(j, carry):
        a, b = carry
        i = steps - 1 - j
        e = dec_ref[pl.ds(pl.multiple_of((i + 1) * segs, segs), segs), :]
        u = up_ref[pl.ds(pl.multiple_of(i * segs, segs), segs), :]
        return (a * e, e * b + u)

    a, b = lax.fori_loop(0, steps, bwd, (ones, zeros), unroll=UNROLL)
    ba_ref[...] = a
    bb_ref[...] = b


def _sweep_kernel(g_ref, gn_ref, r_ref, if_ref, ib_ref, drive_ref, up_ref, st_ref, adj_ref,
                  dec_ref):
    steps, segs, _ = g_ref.shape
    r = r_ref[...]

    def fwd(i, b):
        rows = pl.ds(pl.multiple_of(i * segs, segs), segs)
        d = jnp.exp(-(g_ref[i] * r))
        dec_ref[rows, :] = d
        b = d * b + drive_ref[rows, :]
        st_ref[rows, :] = b
        return b

    lax.fori_loop(0, steps, fwd, if_ref[...], unroll=UNROLL)

    dec_ref[pl.ds(steps * segs, segs), :] = jnp.exp(-(gn_ref[steps - 1] * r))

    def bwd(j, b):
        i = steps - 1 - j
        rows = pl.ds(pl.multiple_of(i * segs, segs), segs)
        e = dec_ref[pl.ds(pl.multiple_of((i + 1) * segs, segs), segs), :]
        b = e * b + up_ref[rows, :]
        adj_ref[rows, :] = b
        return b

    lax.fori_loop(0, steps, bwd, ib_ref[...], unroll=UNROLL)


def _whole(shape):
    return pl.BlockSpec(shape, lambda j: (0,) * len(shape))


def local_summaries(g3, gn3, rates2, drive, up):
    total, width = drive.shape
    steps, segs, _ = g3.shape
    seg_shape = jax.ShapeDtypeStruct((segs, width), jnp.float32)
    return pl.pallas_call(
        _summary_kernel,
        grid=(1,),
        in_specs=[_whole(g3.shape), _whole(gn3.shape), _whole(rates2.shape),
                  _whole(drive.shape), _whole(up.shape)],
        out_specs=[_whole((segs, width))] * 4,
        out_shape=[seg_shape] * 4,
        scratch_shapes=[pltpu.VMEM((total + segs, width), jnp.float32)],
        compiler_params=pltpu.CompilerParams(vmem_limit_bytes=48 * 1024 * 1024),
    )(g3, gn3, rates2, drive, up)


def sweeps(g3, gn3, rates2, drive, up, init_f, init_b):
    total, width = drive.shape
    segs = g3.shape[1]
    full = jax.ShapeDtypeStruct((total, width), jnp.float32)
    return pl.pallas_call(
        _sweep_kernel,
        grid=(1,),
        in_specs=[_whole(g3.shape), _whole(gn3.shape), _whole(rates2.shape),
                  _whole(init_f.shape), _whole(init_b.shape),
                  _whole(drive.shape), _whole(up.shape)],
        out_specs=[_whole(full.shape)] * 2,
        out_shape=[full, full],
        scratch_shapes=[pltpu.VMEM((total + segs, width), jnp.float32)],
        compiler_params=pltpu.CompilerParams(vmem_limit_bytes=48 * 1024 * 1024),
    )(g3, gn3, rates2, init_f, init_b, drive, up)


def _pick(x, index):
    return lax.dynamic_index_in_dim(x, index, 0, keepdims=False)


def chan_reduce(partial_t):
    ys = lax.axis_size("cy")
    cores = lax.axis_size("cc")
    y = lax.axis_index("cy")
    core = lax.axis_index("cc")
    dmodel, total = partial_t.shape
    blk = dmodel // (ys * cores)
    parts = partial_t.reshape(ys, cores, blk, total).transpose(1, 0, 2, 3)
    both = lax.all_to_all(parts, "cc", 0, 0)
    acc = both[0].astype(jnp.float32) + both[1].astype(jnp.float32)
    half = total // 2
    ahead = acc[:, :, :half]
    behind = acc[:, :, half:]
    up_ring = [(i, (i + 1) % ys) for i in range(ys)]
    down_ring = [(i, (i - 1) % ys) for i in range(ys)]
    buf_a = _pick(ahead, (y - 1) % ys)
    buf_b = _pick(behind, (y + 1) % ys)
    for k in range(ys - 1):
        got_a = lax.ppermute(buf_a.astype(jnp.bfloat16), "cy", up_ring)
        got_b = lax.ppermute(buf_b.astype(jnp.bfloat16), "cy", down_ring)
        buf_a = _pick(ahead, (y - k - 2) % ys) + got_a.astype(jnp.float32)
        buf_b = _pick(behind, (y + k + 2) % ys) + got_b.astype(jnp.float32)
    return jnp.concatenate([buf_a, buf_b], 1).astype(jnp.bfloat16)


def local(inputs, gaps, rates, w_in, w_out, cotangent):
    total = inputs.shape[0]
    width = rates.shape[0]
    segs = SEGMENTS
    steps = total // segs
    peers = lax.axis_size(SEQ)
    place = lax.axis_index(SEQ)
    factor = 1.0 / math.sqrt(total * peers)

    def interleave(x):
        return x.reshape((segs, steps) + x.shape[1:]).swapaxes(0, 1).reshape(x.shape)

    x_rows = interleave(inputs)
    c_rows = interleave(cotangent)
    g_rows = interleave(gaps)
    gain = jnp.sqrt(-jnp.expm1(-2.0 * g_rows[:, None] * rates[None, :]))
    drive = gain * jnp.dot(x_rows, w_in, preferred_element_type=jnp.float32)
    upstream = lax.dot_general(
        c_rows, w_out, (((1,), (1,)), ((), ())), preferred_element_type=jnp.float32
    )
    gaps_next = jnp.concatenate([gaps[1:], jnp.zeros((1,), jnp.float32)], 0)
    g3 = g_rows.reshape(steps, segs)[:, :, None]
    gn3 = interleave(gaps_next).reshape(steps, segs)[:, :, None]
    rates2 = rates[None, :]

    fa, fb, ba, bb = local_summaries(g3, gn3, rates2, drive, up=upstream)

    end_state = jnp.zeros((width,), jnp.float32)
    block_decay = jnp.ones((width,), jnp.float32)
    for s in range(segs):
        end_state = fb[s] + fa[s] * end_state
        block_decay = block_decay * fa[s]
    first_adj = jnp.zeros((width,), jnp.float32)
    for s in reversed(range(segs)):
        first_adj = bb[s] + ba[s] * first_adj
    start_adj = jnp.exp(-gaps[0] * rates) * first_adj

    summary = jnp.stack([block_decay, end_state, start_adj], 0)
    gathered = lax.all_gather(lax.all_gather(summary, "sz"), "sx").reshape(peers, 3, width)
    carry_in = jnp.zeros((width,), jnp.float32)
    for q in range(peers):
        new = gathered[q, 1] + gathered[q, 0] * carry_in
        carry_in = jnp.where(q < place, new, carry_in)
    right_in = jnp.zeros((width,), jnp.float32)
    for q in reversed(range(peers)):
        new = gathered[q, 2] + gathered[q, 0] * right_in
        right_in = jnp.where(q > place, new, right_in)

    inits_f = []
    e = carry_in
    for s in range(segs):
        inits_f.append(e)
        e = fb[s] + fa[s] * e
    inits_b = [None] * segs
    v = right_in
    for s in reversed(range(segs)):
        inits_b[s] = v
        v = bb[s] + ba[s] * v
    init_f = jnp.stack(inits_f, 0)
    init_b = jnp.stack(inits_b, 0)

    state, adjoint = sweeps(g3, gn3, rates2, drive, upstream, init_f, init_b)
    drive_grad = (gain * adjoint).astype(jnp.bfloat16)
    state_low = state.astype(jnp.bfloat16)
    in_term = lax.dot_general(
        x_rows, drive_grad, (((0,), (0,)), ((), ())), preferred_element_type=jnp.float32
    ) * factor
    out_term = lax.dot_general(
        c_rows, state_low, (((0,), (0,)), ((), ())), preferred_element_type=jnp.float32
    ) * factor
    joined = jnp.concatenate([in_term, out_term], 1).astype(jnp.bfloat16)
    joined = lax.psum_scatter(joined, "sx", scatter_dimension=0, tiled=True)
    joined = lax.psum_scatter(joined, "sz", scatter_dimension=0, tiled=True).astype(jnp.float32)
    d_w_in = joined[:, :width]
    d_w_out = joined[:, width:].T
    partial_t = lax.dot_general(
        w_in, drive_grad, (((1,), (1,)), ((), ())), preferred_element_type=jnp.float32
    ).astype(jnp.bfloat16)
    d_rows = chan_reduce(partial_t).T
    d_inputs = d_rows.reshape((steps, segs) + d_rows.shape[1:]).swapaxes(0, 1).reshape(d_rows.shape)
    return (d_inputs, d_w_in, d_w_out)


SEQ = ("sx", "sz")
CHAN = ("cy", "cc")


def solution(mesh):
    grid = mesh.devices
    seq_size, chan_size = grid.shape
    z_size = len({d.coords[2] for d in grid[:, 0]})
    core_size = len({d.core_on_chip for d in grid[0, :]})
    split = Mesh(
        grid.reshape(seq_size // z_size, z_size, chan_size // core_size, core_size),
        ("sx", "sz", "cy", "cc"),
    )
    placed = (P(SEQ, None), P(SEQ), P(CHAN), P(None, CHAN), P(CHAN, None), P(SEQ, None))
    return jax.shard_map(
        local,
        mesh=split,
        in_specs=placed,
        out_specs=(P(SEQ, CHAN), P(SEQ, CHAN), P(CHAN, SEQ)),
        check_vma=False,
    )
```

```python
import math

import jax
import jax.numpy as jnp
from jax import lax
from jax.experimental import pallas as pl
from jax.experimental.pallas import tpu as pltpu
from jax.sharding import Mesh, PartitionSpec as P

SEGMENTS = 8
LANES = 128
UNROLL = 16


def _summary_kernel(g_ref, gn_ref, r_ref, drive_ref, up_ref, fa_ref, fb_ref, ba_ref, bb_ref,
                    dec_ref):
    steps, segs, _ = g_ref.shape
    r = r_ref[...]
    ones = jnp.ones(fa_ref.shape, jnp.float32)
    zeros = jnp.zeros(fb_ref.shape, jnp.float32)

    def fwd(i, carry):
        a, b = carry
        rows = pl.ds(pl.multiple_of(i * segs, segs), segs)
        d = jnp.exp(-(g_ref[i] * r))
        dec_ref[rows, :] = d
        x = drive_ref[rows, :]
        return (a * d, d * b + x)

    a, b = lax.fori_loop(0, steps, fwd, (ones, zeros), unroll=UNROLL)
    fa_ref[...] = a
    fb_ref[...] = b

    dec_ref[pl.ds(steps * segs, segs), :] = jnp.exp(-(gn_ref[steps - 1] * r))

    def bwd(j, carry):
        a, b = carry
        i = steps - 1 - j
        e = dec_ref[pl.ds(pl.multiple_of((i + 1) * segs, segs), segs), :]
        u = up_ref[pl.ds(pl.multiple_of(i * segs, segs), segs), :]
        return (a * e, e * b + u)

    a, b = lax.fori_loop(0, steps, bwd, (ones, zeros), unroll=UNROLL)
    ba_ref[...] = a
    bb_ref[...] = b


def _sweep_kernel(g_ref, gn_ref, r_ref, if_ref, ib_ref, drive_ref, up_ref, st_ref, adj_ref,
                  dec_ref):
    steps, segs, _ = g_ref.shape
    r = r_ref[...]

    def fwd(i, b):
        rows = pl.ds(pl.multiple_of(i * segs, segs), segs)
        d = jnp.exp(-(g_ref[i] * r))
        dec_ref[rows, :] = d
        b = d * b + drive_ref[rows, :]
        st_ref[rows, :] = b
        return b

    lax.fori_loop(0, steps, fwd, if_ref[...], unroll=UNROLL)

    dec_ref[pl.ds(steps * segs, segs), :] = jnp.exp(-(gn_ref[steps - 1] * r))

    def bwd(j, b):
        i = steps - 1 - j
        rows = pl.ds(pl.multiple_of(i * segs, segs), segs)
        e = dec_ref[pl.ds(pl.multiple_of((i + 1) * segs, segs), segs), :]
        b = e * b + up_ref[rows, :]
        adj_ref[rows, :] = b
        return b

    lax.fori_loop(0, steps, bwd, ib_ref[...], unroll=UNROLL)


def _whole(shape):
    return pl.BlockSpec(shape, lambda j: (0,) * len(shape))


def local_summaries(g3, gn3, rates2, drive, up):
    total, width = drive.shape
    steps, segs, _ = g3.shape
    seg_shape = jax.ShapeDtypeStruct((segs, width), jnp.float32)
    return pl.pallas_call(
        _summary_kernel,
        grid=(1,),
        in_specs=[_whole(g3.shape), _whole(gn3.shape), _whole(rates2.shape),
                  _whole(drive.shape), _whole(up.shape)],
        out_specs=[_whole((segs, width))] * 4,
        out_shape=[seg_shape] * 4,
        scratch_shapes=[pltpu.VMEM((total + segs, width), jnp.float32)],
        compiler_params=pltpu.CompilerParams(vmem_limit_bytes=48 * 1024 * 1024),
    )(g3, gn3, rates2, drive, up)


def sweeps(g3, gn3, rates2, drive, up, init_f, init_b):
    total, width = drive.shape
    segs = g3.shape[1]
    full = jax.ShapeDtypeStruct((total, width), jnp.float32)
    return pl.pallas_call(
        _sweep_kernel,
        grid=(1,),
        in_specs=[_whole(g3.shape), _whole(gn3.shape), _whole(rates2.shape),
                  _whole(init_f.shape), _whole(init_b.shape),
                  _whole(drive.shape), _whole(up.shape)],
        out_specs=[_whole(full.shape)] * 2,
        out_shape=[full, full],
        scratch_shapes=[pltpu.VMEM((total + segs, width), jnp.float32)],
        compiler_params=pltpu.CompilerParams(vmem_limit_bytes=48 * 1024 * 1024),
    )(g3, gn3, rates2, init_f, init_b, drive, up)


def _pick(x, index):
    return lax.dynamic_index_in_dim(x, index, 0, keepdims=False)


def chan_reduce(partial_t):
    ys = lax.axis_size("cy")
    cores = lax.axis_size("cc")
    y = lax.axis_index("cy")
    core = lax.axis_index("cc")
    dmodel, total = partial_t.shape
    blk = dmodel // (ys * cores)
    parts = partial_t.reshape(ys, cores, blk, total).transpose(1, 0, 2, 3)
    mine = _pick(parts, core).astype(jnp.float32)
    other = _pick(parts, (core + 1) % cores)
    swap = [(i, (i + 1) % cores) for i in range(cores)]
    acc = mine + lax.ppermute(other, "cc", swap).astype(jnp.float32)
    half = total // 2
    ahead = acc[:, :, :half]
    behind = acc[:, :, half:]
    up_ring = [(i, (i + 1) % ys) for i in range(ys)]
    down_ring = [(i, (i - 1) % ys) for i in range(ys)]
    buf_a = _pick(ahead, (y - 1) % ys)
    buf_b = _pick(behind, (y + 1) % ys)
    for k in range(ys - 1):
        got_a = lax.ppermute(buf_a.astype(jnp.bfloat16), "cy", up_ring)
        got_b = lax.ppermute(buf_b.astype(jnp.bfloat16), "cy", down_ring)
        buf_a = _pick(ahead, (y - k - 2) % ys) + got_a.astype(jnp.float32)
        buf_b = _pick(behind, (y + k + 2) % ys) + got_b.astype(jnp.float32)
    return jnp.concatenate([buf_a, buf_b], 1).astype(jnp.bfloat16)


def local(inputs, gaps, rates, w_in, w_out, cotangent):
    total = inputs.shape[0]
    width = rates.shape[0]
    segs = SEGMENTS
    steps = total // segs
    peers = lax.axis_size(SEQ)
    place = lax.axis_index(SEQ)
    factor = 1.0 / math.sqrt(total * peers)

    def interleave(x):
        return x.reshape((segs, steps) + x.shape[1:]).swapaxes(0, 1).reshape(x.shape)

    x_rows = interleave(inputs)
    c_rows = interleave(cotangent)
    g_rows = interleave(gaps)
    gain = jnp.sqrt(-jnp.expm1(-2.0 * g_rows[:, None] * rates[None, :]))
    drive = gain * jnp.dot(x_rows, w_in, preferred_element_type=jnp.float32)
    upstream = lax.dot_general(
        c_rows, w_out, (((1,), (1,)), ((), ())), preferred_element_type=jnp.float32
    )
    gaps_next = jnp.concatenate([gaps[1:], jnp.zeros((1,), jnp.float32)], 0)
    g3 = g_rows.reshape(steps, segs)[:, :, None]
    gn3 = interleave(gaps_next).reshape(steps, segs)[:, :, None]
    rates2 = rates[None, :]

    fa, fb, ba, bb = local_summaries(g3, gn3, rates2, drive, up=upstream)

    end_state = jnp.zeros((width,), jnp.float32)
    block_decay = jnp.ones((width,), jnp.float32)
    for s in range(segs):
        end_state = fb[s] + fa[s] * end_state
        block_decay = block_decay * fa[s]
    first_adj = jnp.zeros((width,), jnp.float32)
    for s in reversed(range(segs)):
        first_adj = bb[s] + ba[s] * first_adj
    start_adj = jnp.exp(-gaps[0] * rates) * first_adj

    summary = jnp.stack([block_decay, end_state, start_adj], 0)
    gathered = lax.all_gather(lax.all_gather(summary, "sz"), "sx").reshape(peers, 3, width)
    carry_in = jnp.zeros((width,), jnp.float32)
    for q in range(peers):
        new = gathered[q, 1] + gathered[q, 0] * carry_in
        carry_in = jnp.where(q < place, new, carry_in)
    right_in = jnp.zeros((width,), jnp.float32)
    for q in reversed(range(peers)):
        new = gathered[q, 2] + gathered[q, 0] * right_in
        right_in = jnp.where(q > place, new, right_in)

    inits_f = []
    e = carry_in
    for s in range(segs):
        inits_f.append(e)
        e = fb[s] + fa[s] * e
    inits_b = [None] * segs
    v = right_in
    for s in reversed(range(segs)):
        inits_b[s] = v
        v = bb[s] + ba[s] * v
    init_f = jnp.stack(inits_f, 0)
    init_b = jnp.stack(inits_b, 0)

    state, adjoint = sweeps(g3, gn3, rates2, drive, upstream, init_f, init_b)
    drive_grad = (gain * adjoint).astype(jnp.bfloat16)
    state_low = state.astype(jnp.bfloat16)
    in_term = lax.dot_general(
        x_rows, drive_grad, (((0,), (0,)), ((), ())), preferred_element_type=jnp.float32
    ) * factor
    out_term = lax.dot_general(
        c_rows, state_low, (((0,), (0,)), ((), ())), preferred_element_type=jnp.float32
    ) * factor
    joined = jnp.concatenate([in_term, out_term], 1).astype(jnp.bfloat16)
    joined = lax.psum_scatter(joined, "sx", scatter_dimension=0, tiled=True)
    joined = lax.psum_scatter(joined, "sz", scatter_dimension=0, tiled=True).astype(jnp.float32)
    d_w_in = joined[:, :width]
    d_w_out = joined[:, width:].T
    partial_t = lax.dot_general(
        w_in, drive_grad, (((1,), (1,)), ((), ())), preferred_element_type=jnp.float32
    ).astype(jnp.bfloat16)
    d_rows = chan_reduce(partial_t).T
    d_inputs = d_rows.reshape((steps, segs) + d_rows.shape[1:]).swapaxes(0, 1).reshape(d_rows.shape)
    return (d_inputs, d_w_in, d_w_out)


SEQ = ("sx", "sz")
CHAN = ("cy", "cc")


def solution(mesh):
    grid = mesh.devices
    seq_size, chan_size = grid.shape
    z_size = len({d.coords[2] for d in grid[:, 0]})
    core_size = len({d.core_on_chip for d in grid[0, :]})
    split = Mesh(
        grid.reshape(seq_size // z_size, z_size, chan_size // core_size, core_size),
        ("sx", "sz", "cy", "cc"),
    )
    placed = (P(SEQ, None), P(SEQ), P(CHAN), P(None, CHAN), P(CHAN, None), P(SEQ, None))
    return jax.shard_map(
        local,
        mesh=split,
        in_specs=placed,
        out_specs=(P(SEQ, CHAN), P(SEQ, CHAN), P(CHAN, SEQ)),
        check_vma=False,
    )
```

```python
import math

import jax
import jax.numpy as jnp
from jax import lax
from jax.experimental import pallas as pl
from jax.experimental.pallas import tpu as pltpu
from jax.sharding import Mesh, PartitionSpec as P

SEGMENTS = 8
LANES = 128
UNROLL = 32


def _summary_kernel(g_ref, gn_ref, r_ref, drive_ref, up_ref, fa_ref, fb_ref, ba_ref, bb_ref,
                    dec_ref):
    steps, segs, _ = g_ref.shape
    r = r_ref[...]
    ones = jnp.ones(fa_ref.shape, jnp.float32)
    zeros = jnp.zeros(fb_ref.shape, jnp.float32)

    def fwd(i, carry):
        a, b = carry
        rows = pl.ds(pl.multiple_of(i * segs, segs), segs)
        d = jnp.exp(-(g_ref[i] * r))
        dec_ref[rows, :] = d
        x = drive_ref[rows, :]
        return (a * d, d * b + x)

    a, b = lax.fori_loop(0, steps, fwd, (ones, zeros), unroll=UNROLL)
    fa_ref[...] = a
    fb_ref[...] = b

    dec_ref[pl.ds(steps * segs, segs), :] = jnp.exp(-(gn_ref[steps - 1] * r))

    def bwd(j, carry):
        a, b = carry
        i = steps - 1 - j
        e = dec_ref[pl.ds(pl.multiple_of((i + 1) * segs, segs), segs), :]
        u = up_ref[pl.ds(pl.multiple_of(i * segs, segs), segs), :]
        return (a * e, e * b + u)

    a, b = lax.fori_loop(0, steps, bwd, (ones, zeros), unroll=UNROLL)
    ba_ref[...] = a
    bb_ref[...] = b


def _sweep_kernel(g_ref, gn_ref, r_ref, if_ref, ib_ref, drive_ref, up_ref, st_ref, adj_ref,
                  dec_ref):
    steps, segs, _ = g_ref.shape
    r = r_ref[...]

    def fwd(i, b):
        rows = pl.ds(pl.multiple_of(i * segs, segs), segs)
        d = jnp.exp(-(g_ref[i] * r))
        dec_ref[rows, :] = d
        b = d * b + drive_ref[rows, :]
        st_ref[rows, :] = b
        return b

    lax.fori_loop(0, steps, fwd, if_ref[...], unroll=UNROLL)

    dec_ref[pl.ds(steps * segs, segs), :] = jnp.exp(-(gn_ref[steps - 1] * r))

    def bwd(j, b):
        i = steps - 1 - j
        rows = pl.ds(pl.multiple_of(i * segs, segs), segs)
        e = dec_ref[pl.ds(pl.multiple_of((i + 1) * segs, segs), segs), :]
        b = e * b + up_ref[rows, :]
        adj_ref[rows, :] = b
        return b

    lax.fori_loop(0, steps, bwd, ib_ref[...], unroll=UNROLL)


def _whole(shape):
    return pl.BlockSpec(shape, lambda j: (0,) * len(shape))


def local_summaries(g3, gn3, rates2, drive, up):
    total, width = drive.shape
    steps, segs, _ = g3.shape
    seg_shape = jax.ShapeDtypeStruct((segs, width), jnp.float32)
    return pl.pallas_call(
        _summary_kernel,
        grid=(1,),
        in_specs=[_whole(g3.shape), _whole(gn3.shape), _whole(rates2.shape),
                  _whole(drive.shape), _whole(up.shape)],
        out_specs=[_whole((segs, width))] * 4,
        out_shape=[seg_shape] * 4,
        scratch_shapes=[pltpu.VMEM((total + segs, width), jnp.float32)],
        compiler_params=pltpu.CompilerParams(vmem_limit_bytes=48 * 1024 * 1024),
    )(g3, gn3, rates2, drive, up)


def sweeps(g3, gn3, rates2, drive, up, init_f, init_b):
    total, width = drive.shape
    segs = g3.shape[1]
    full = jax.ShapeDtypeStruct((total, width), jnp.float32)
    return pl.pallas_call(
        _sweep_kernel,
        grid=(1,),
        in_specs=[_whole(g3.shape), _whole(gn3.shape), _whole(rates2.shape),
                  _whole(init_f.shape), _whole(init_b.shape),
                  _whole(drive.shape), _whole(up.shape)],
        out_specs=[_whole(full.shape)] * 2,
        out_shape=[full, full],
        scratch_shapes=[pltpu.VMEM((total + segs, width), jnp.float32)],
        compiler_params=pltpu.CompilerParams(vmem_limit_bytes=48 * 1024 * 1024),
    )(g3, gn3, rates2, init_f, init_b, drive, up)


def _pick(x, index):
    return lax.dynamic_index_in_dim(x, index, 0, keepdims=False)


def chan_reduce(partial_t):
    ys = lax.axis_size("cy")
    cores = lax.axis_size("cc")
    y = lax.axis_index("cy")
    core = lax.axis_index("cc")
    dmodel, total = partial_t.shape
    blk = dmodel // (ys * cores)
    parts = partial_t.reshape(ys, cores, blk, total).transpose(1, 0, 2, 3)
    mine = _pick(parts, core).astype(jnp.float32)
    other = _pick(parts, (core + 1) % cores)
    swap = [(i, (i + 1) % cores) for i in range(cores)]
    acc = mine + lax.ppermute(other, "cc", swap).astype(jnp.float32)
    half = total // 2
    ahead = acc[:, :, :half]
    behind = acc[:, :, half:]
    up_ring = [(i, (i + 1) % ys) for i in range(ys)]
    down_ring = [(i, (i - 1) % ys) for i in range(ys)]
    buf_a = _pick(ahead, (y - 1) % ys)
    buf_b = _pick(behind, (y + 1) % ys)
    for k in range(ys - 1):
        got_a = lax.ppermute(buf_a.astype(jnp.bfloat16), "cy", up_ring)
        got_b = lax.ppermute(buf_b.astype(jnp.bfloat16), "cy", down_ring)
        buf_a = _pick(ahead, (y - k - 2) % ys) + got_a.astype(jnp.float32)
        buf_b = _pick(behind, (y + k + 2) % ys) + got_b.astype(jnp.float32)
    return jnp.concatenate([buf_a, buf_b], 1).astype(jnp.bfloat16)


def local(inputs, gaps, rates, w_in, w_out, cotangent):
    total = inputs.shape[0]
    width = rates.shape[0]
    segs = SEGMENTS
    steps = total // segs
    peers = lax.axis_size(SEQ)
    place = lax.axis_index(SEQ)
    factor = 1.0 / math.sqrt(total * peers)

    def interleave(x):
        return x.reshape((segs, steps) + x.shape[1:]).swapaxes(0, 1).reshape(x.shape)

    x_rows = interleave(inputs)
    c_rows = interleave(cotangent)
    g_rows = interleave(gaps)
    gain = jnp.sqrt(-jnp.expm1(-2.0 * g_rows[:, None] * rates[None, :]))
    drive = gain * jnp.dot(x_rows, w_in, preferred_element_type=jnp.float32)
    upstream = lax.dot_general(
        c_rows, w_out, (((1,), (1,)), ((), ())), preferred_element_type=jnp.float32
    )
    gaps_next = jnp.concatenate([gaps[1:], jnp.zeros((1,), jnp.float32)], 0)
    g3 = g_rows.reshape(steps, segs)[:, :, None]
    gn3 = interleave(gaps_next).reshape(steps, segs)[:, :, None]
    rates2 = rates[None, :]

    fa, fb, ba, bb = local_summaries(g3, gn3, rates2, drive, up=upstream)

    end_state = jnp.zeros((width,), jnp.float32)
    block_decay = jnp.ones((width,), jnp.float32)
    for s in range(segs):
        end_state = fb[s] + fa[s] * end_state
        block_decay = block_decay * fa[s]
    first_adj = jnp.zeros((width,), jnp.float32)
    for s in reversed(range(segs)):
        first_adj = bb[s] + ba[s] * first_adj
    start_adj = jnp.exp(-gaps[0] * rates) * first_adj

    summary = jnp.stack([block_decay, end_state, start_adj], 0)
    gathered = lax.all_gather(lax.all_gather(summary, "sz"), "sx").reshape(peers, 3, width)
    carry_in = jnp.zeros((width,), jnp.float32)
    for q in range(peers):
        new = gathered[q, 1] + gathered[q, 0] * carry_in
        carry_in = jnp.where(q < place, new, carry_in)
    right_in = jnp.zeros((width,), jnp.float32)
    for q in reversed(range(peers)):
        new = gathered[q, 2] + gathered[q, 0] * right_in
        right_in = jnp.where(q > place, new, right_in)

    inits_f = []
    e = carry_in
    for s in range(segs):
        inits_f.append(e)
        e = fb[s] + fa[s] * e
    inits_b = [None] * segs
    v = right_in
    for s in reversed(range(segs)):
        inits_b[s] = v
        v = bb[s] + ba[s] * v
    init_f = jnp.stack(inits_f, 0)
    init_b = jnp.stack(inits_b, 0)

    state, adjoint = sweeps(g3, gn3, rates2, drive, upstream, init_f, init_b)
    drive_grad = (gain * adjoint).astype(jnp.bfloat16)
    state_low = state.astype(jnp.bfloat16)
    in_term = lax.dot_general(
        x_rows, drive_grad, (((0,), (0,)), ((), ())), preferred_element_type=jnp.float32
    ) * factor
    out_term = lax.dot_general(
        c_rows, state_low, (((0,), (0,)), ((), ())), preferred_element_type=jnp.float32
    ) * factor
    joined = jnp.concatenate([in_term, out_term], 1).astype(jnp.bfloat16)
    joined = lax.psum_scatter(joined, "sx", scatter_dimension=0, tiled=True)
    joined = lax.psum_scatter(joined, "sz", scatter_dimension=0, tiled=True).astype(jnp.float32)
    d_w_in = joined[:, :width]
    d_w_out = joined[:, width:].T
    partial_t = lax.dot_general(
        w_in, drive_grad, (((1,), (1,)), ((), ())), preferred_element_type=jnp.float32
    ).astype(jnp.bfloat16)
    d_rows = chan_reduce(partial_t).T
    d_inputs = d_rows.reshape((steps, segs) + d_rows.shape[1:]).swapaxes(0, 1).reshape(d_rows.shape)
    return (d_inputs, d_w_in, d_w_out)


SEQ = ("sx", "sz")
CHAN = ("cy", "cc")


def solution(mesh):
    grid = mesh.devices
    seq_size, chan_size = grid.shape
    z_size = len({d.coords[2] for d in grid[:, 0]})
    core_size = len({d.core_on_chip for d in grid[0, :]})
    split = Mesh(
        grid.reshape(seq_size // z_size, z_size, chan_size // core_size, core_size),
        ("sx", "sz", "cy", "cc"),
    )
    placed = (P(SEQ, None), P(SEQ), P(CHAN), P(None, CHAN), P(CHAN, None), P(SEQ, None))
    return jax.shard_map(
        local,
        mesh=split,
        in_specs=placed,
        out_specs=(P(SEQ, CHAN), P(SEQ, CHAN), P(CHAN, SEQ)),
        check_vma=False,
    )
```

```python
import math

import jax
import jax.numpy as jnp
from jax import lax
from jax.experimental import pallas as pl
from jax.experimental.pallas import tpu as pltpu
from jax.sharding import Mesh, PartitionSpec as P

SEGMENTS = 8
LANES = 128
UNROLL = 64


def _summary_kernel(g_ref, gn_ref, r_ref, drive_ref, up_ref, fa_ref, fb_ref, ba_ref, bb_ref,
                    dec_ref):
    steps, segs, _ = g_ref.shape
    r = r_ref[...]
    ones = jnp.ones(fa_ref.shape, jnp.float32)
    zeros = jnp.zeros(fb_ref.shape, jnp.float32)

    def fwd(i, carry):
        a, b = carry
        rows = pl.ds(pl.multiple_of(i * segs, segs), segs)
        d = jnp.exp(-(g_ref[i] * r))
        dec_ref[rows, :] = d
        x = drive_ref[rows, :]
        return (a * d, d * b + x)

    a, b = lax.fori_loop(0, steps, fwd, (ones, zeros), unroll=UNROLL)
    fa_ref[...] = a
    fb_ref[...] = b

    dec_ref[pl.ds(steps * segs, segs), :] = jnp.exp(-(gn_ref[steps - 1] * r))

    def bwd(j, carry):
        a, b = carry
        i = steps - 1 - j
        e = dec_ref[pl.ds(pl.multiple_of((i + 1) * segs, segs), segs), :]
        u = up_ref[pl.ds(pl.multiple_of(i * segs, segs), segs), :]
        return (a * e, e * b + u)

    a, b = lax.fori_loop(0, steps, bwd, (ones, zeros), unroll=UNROLL)
    ba_ref[...] = a
    bb_ref[...] = b


def _sweep_kernel(g_ref, gn_ref, r_ref, if_ref, ib_ref, drive_ref, up_ref, st_ref, adj_ref,
                  dec_ref):
    steps, segs, _ = g_ref.shape
    r = r_ref[...]

    def fwd(i, b):
        rows = pl.ds(pl.multiple_of(i * segs, segs), segs)
        d = jnp.exp(-(g_ref[i] * r))
        dec_ref[rows, :] = d
        b = d * b + drive_ref[rows, :]
        st_ref[rows, :] = b
        return b

    lax.fori_loop(0, steps, fwd, if_ref[...], unroll=UNROLL)

    dec_ref[pl.ds(steps * segs, segs), :] = jnp.exp(-(gn_ref[steps - 1] * r))

    def bwd(j, b):
        i = steps - 1 - j
        rows = pl.ds(pl.multiple_of(i * segs, segs), segs)
        e = dec_ref[pl.ds(pl.multiple_of((i + 1) * segs, segs), segs), :]
        b = e * b + up_ref[rows, :]
        adj_ref[rows, :] = b
        return b

    lax.fori_loop(0, steps, bwd, ib_ref[...], unroll=UNROLL)


def _whole(shape):
    return pl.BlockSpec(shape, lambda j: (0,) * len(shape))


def local_summaries(g3, gn3, rates2, drive, up):
    total, width = drive.shape
    steps, segs, _ = g3.shape
    seg_shape = jax.ShapeDtypeStruct((segs, width), jnp.float32)
    return pl.pallas_call(
        _summary_kernel,
        grid=(1,),
        in_specs=[_whole(g3.shape), _whole(gn3.shape), _whole(rates2.shape),
                  _whole(drive.shape), _whole(up.shape)],
        out_specs=[_whole((segs, width))] * 4,
        out_shape=[seg_shape] * 4,
        scratch_shapes=[pltpu.VMEM((total + segs, width), jnp.float32)],
        compiler_params=pltpu.CompilerParams(vmem_limit_bytes=48 * 1024 * 1024),
    )(g3, gn3, rates2, drive, up)


def sweeps(g3, gn3, rates2, drive, up, init_f, init_b):
    total, width = drive.shape
    segs = g3.shape[1]
    full = jax.ShapeDtypeStruct((total, width), jnp.float32)
    return pl.pallas_call(
        _sweep_kernel,
        grid=(1,),
        in_specs=[_whole(g3.shape), _whole(gn3.shape), _whole(rates2.shape),
                  _whole(init_f.shape), _whole(init_b.shape),
                  _whole(drive.shape), _whole(up.shape)],
        out_specs=[_whole(full.shape)] * 2,
        out_shape=[full, full],
        scratch_shapes=[pltpu.VMEM((total + segs, width), jnp.float32)],
        compiler_params=pltpu.CompilerParams(vmem_limit_bytes=48 * 1024 * 1024),
    )(g3, gn3, rates2, init_f, init_b, drive, up)


def _pick(x, index):
    return lax.dynamic_index_in_dim(x, index, 0, keepdims=False)


def chan_reduce(partial_t):
    ys = lax.axis_size("cy")
    cores = lax.axis_size("cc")
    y = lax.axis_index("cy")
    core = lax.axis_index("cc")
    dmodel, total = partial_t.shape
    blk = dmodel // (ys * cores)
    parts = partial_t.reshape(ys, cores, blk, total).transpose(1, 0, 2, 3)
    mine = _pick(parts, core).astype(jnp.float32)
    other = _pick(parts, (core + 1) % cores)
    swap = [(i, (i + 1) % cores) for i in range(cores)]
    acc = mine + lax.ppermute(other, "cc", swap).astype(jnp.float32)
    half = total // 2
    ahead = acc[:, :, :half]
    behind = acc[:, :, half:]
    up_ring = [(i, (i + 1) % ys) for i in range(ys)]
    down_ring = [(i, (i - 1) % ys) for i in range(ys)]
    buf_a = _pick(ahead, (y - 1) % ys)
    buf_b = _pick(behind, (y + 1) % ys)
    for k in range(ys - 1):
        got_a = lax.ppermute(buf_a.astype(jnp.bfloat16), "cy", up_ring)
        got_b = lax.ppermute(buf_b.astype(jnp.bfloat16), "cy", down_ring)
        buf_a = _pick(ahead, (y - k - 2) % ys) + got_a.astype(jnp.float32)
        buf_b = _pick(behind, (y + k + 2) % ys) + got_b.astype(jnp.float32)
    return jnp.concatenate([buf_a, buf_b], 1).astype(jnp.bfloat16)


def local(inputs, gaps, rates, w_in, w_out, cotangent):
    total = inputs.shape[0]
    width = rates.shape[0]
    segs = SEGMENTS
    steps = total // segs
    peers = lax.axis_size(SEQ)
    place = lax.axis_index(SEQ)
    factor = 1.0 / math.sqrt(total * peers)

    def interleave(x):
        return x.reshape((segs, steps) + x.shape[1:]).swapaxes(0, 1).reshape(x.shape)

    x_rows = interleave(inputs)
    c_rows = interleave(cotangent)
    g_rows = interleave(gaps)
    gain = jnp.sqrt(-jnp.expm1(-2.0 * g_rows[:, None] * rates[None, :]))
    drive = gain * jnp.dot(x_rows, w_in, preferred_element_type=jnp.float32)
    upstream = lax.dot_general(
        c_rows, w_out, (((1,), (1,)), ((), ())), preferred_element_type=jnp.float32
    )
    gaps_next = jnp.concatenate([gaps[1:], jnp.zeros((1,), jnp.float32)], 0)
    g3 = g_rows.reshape(steps, segs)[:, :, None]
    gn3 = interleave(gaps_next).reshape(steps, segs)[:, :, None]
    rates2 = rates[None, :]

    fa, fb, ba, bb = local_summaries(g3, gn3, rates2, drive, up=upstream)

    end_state = jnp.zeros((width,), jnp.float32)
    block_decay = jnp.ones((width,), jnp.float32)
    for s in range(segs):
        end_state = fb[s] + fa[s] * end_state
        block_decay = block_decay * fa[s]
    first_adj = jnp.zeros((width,), jnp.float32)
    for s in reversed(range(segs)):
        first_adj = bb[s] + ba[s] * first_adj
    start_adj = jnp.exp(-gaps[0] * rates) * first_adj

    summary = jnp.stack([block_decay, end_state, start_adj], 0)
    gathered = lax.all_gather(lax.all_gather(summary, "sz"), "sx").reshape(peers, 3, width)
    carry_in = jnp.zeros((width,), jnp.float32)
    for q in range(peers):
        new = gathered[q, 1] + gathered[q, 0] * carry_in
        carry_in = jnp.where(q < place, new, carry_in)
    right_in = jnp.zeros((width,), jnp.float32)
    for q in reversed(range(peers)):
        new = gathered[q, 2] + gathered[q, 0] * right_in
        right_in = jnp.where(q > place, new, right_in)

    inits_f = []
    e = carry_in
    for s in range(segs):
        inits_f.append(e)
        e = fb[s] + fa[s] * e
    inits_b = [None] * segs
    v = right_in
    for s in reversed(range(segs)):
        inits_b[s] = v
        v = bb[s] + ba[s] * v
    init_f = jnp.stack(inits_f, 0)
    init_b = jnp.stack(inits_b, 0)

    state, adjoint = sweeps(g3, gn3, rates2, drive, upstream, init_f, init_b)
    drive_grad = (gain * adjoint).astype(jnp.bfloat16)
    state_low = state.astype(jnp.bfloat16)
    in_term = lax.dot_general(
        x_rows, drive_grad, (((0,), (0,)), ((), ())), preferred_element_type=jnp.float32
    ) * factor
    out_term = lax.dot_general(
        c_rows, state_low, (((0,), (0,)), ((), ())), preferred_element_type=jnp.float32
    ) * factor
    joined = jnp.concatenate([in_term, out_term], 1).astype(jnp.bfloat16)
    joined = lax.psum_scatter(joined, "sx", scatter_dimension=0, tiled=True)
    joined = lax.psum_scatter(joined, "sz", scatter_dimension=0, tiled=True).astype(jnp.float32)
    d_w_in = joined[:, :width]
    d_w_out = joined[:, width:].T
    partial_t = lax.dot_general(
        w_in, drive_grad, (((1,), (1,)), ((), ())), preferred_element_type=jnp.float32
    ).astype(jnp.bfloat16)
    d_rows = chan_reduce(partial_t).T
    d_inputs = d_rows.reshape((steps, segs) + d_rows.shape[1:]).swapaxes(0, 1).reshape(d_rows.shape)
    return (d_inputs, d_w_in, d_w_out)


SEQ = ("sx", "sz")
CHAN = ("cy", "cc")


def solution(mesh):
    grid = mesh.devices
    seq_size, chan_size = grid.shape
    z_size = len({d.coords[2] for d in grid[:, 0]})
    core_size = len({d.core_on_chip for d in grid[0, :]})
    split = Mesh(
        grid.reshape(seq_size // z_size, z_size, chan_size // core_size, core_size),
        ("sx", "sz", "cy", "cc"),
    )
    placed = (P(SEQ, None), P(SEQ), P(CHAN), P(None, CHAN), P(CHAN, None), P(SEQ, None))
    return jax.shard_map(
        local,
        mesh=split,
        in_specs=placed,
        out_specs=(P(SEQ, CHAN), P(SEQ, CHAN), P(CHAN, SEQ)),
        check_vma=False,
    )
```
